512 devices in a mesh: req: 64 (over y, x, core), tp: 8 (over z).
Axes of the slice: x: 4, y: 8, z: 8, core: 2. Of those that a mesh axis runs over, the one named last changes fastest.
Arguments:
- hidden: bfloat16 [2048, 5, 2560], P('req', None, 'tp'), may hold values from -6 to 6
- norm_gain: bfloat16 [2560], replicated, may hold values from 0.099609375 to 1.8984375
- query_weight: bfloat16 [2560, 2560], P(None, 'tp'), may hold values from -0.125 to 0.125
- key_value_matrix: bfloat16 [2560, 8, 160], P(None, 'tp'), may hold values from -0.125 to 0.125
- output_weight: bfloat16 [2560, 2560], P('tp'), may hold values from -0.5 to 0.5
- key_value_cache: bfloat16 [2048, 64, 8, 160], P('req', None, 'tp'), as said below
- deal_order: int32 [2048], P('req'), may hold values from 0 to 2047, as said below
- cache_length: int32 [2048], P('req'), may hold values from 1 to 64, as said below
- accepted: int32 [2048], P('req'), may hold values from 1 to 5
Outputs:
- block_output: bfloat16 [2048, 5, 2560], P('req', None, 'tp')
- new_entries: bfloat16 [2048, 5, 8, 160], P('req', None, 'tp')
The draws below stay inside these ranges and needn't reach their ends.
Inputs may be any that keep to these rules, and one draw needn't show every extreme that they name: deal_order is a permutation of the 2048 requests; slot i lies on index i // 32 of req, and request r arrives on index r // 32. Every index deals at most 1 of its requests to any one index, and exactly 1 to each of 32 indices. Cache entries of slot i at positions from cache_length[i] on are unused. `key_value_cache`: at positions below cache_length[i] the first 80 entries of each head are the keys, already rotated for their positions, and the last 80 the values.
All inputs are finite; a program needn't handle non-finite values.
Results may differ from the reference program's by a relative error of at most 0.0091.
Values may be sent and summed in bfloat16 or wider, within the bound.
No kernel may reach another device: no remote copies, remote signals or barrier semaphores. Data moves between devices by JAX's collectives and lax.ppermute only.
A program may use at most 128 MiB of HBM per device.

```python
import jax
import jax.numpy as jnp
from jax import lax

MODEL_WIDTH = 2560
HQ = 32
KEY_VALUE_HEADS = 8
HEAD_SIZE = 80
VERIFIED_TOKENS = 5
R_DEV = 32
CACHE_SLOTS = 64
HEADS_PER_GROUP = 4
REQUEST_TOTAL = 2048


def draw_key_value_cache(key, part):
    first_key = jax.random.fold_in(key, 11)
    array_extent = (REQUEST_TOTAL, CACHE_SLOTS, KEY_VALUE_HEADS, 2 * HEAD_SIZE)
    return jax.random.normal(first_key, array_extent, jnp.float32).astype(jnp.bfloat16)


def draw_deal_order(key, part):
    peer_count = REQUEST_TOTAL // R_DEV
    first_key = jax.random.fold_in(key, 21)
    second_key = jax.random.fold_in(key, 22)
    third_key = jax.random.fold_in(key, 23)
    mapping = jax.random.permutation(first_key, peer_count)
    offsets = jax.random.permutation(second_key, peer_count)
    rotation = jax.random.randint(third_key, (peer_count,), 0, R_DEV)
    source = jnp.arange(peer_count, dtype=jnp.int32)[:, None]
    local = jnp.arange(R_DEV, dtype=jnp.int32)[None, :]
    target = mapping[(source + offsets[local % peer_count]) % peer_count]
    position = (local + rotation[target]) % R_DEV
    slot_index = (target * R_DEV + position).reshape(-1)
    request = (source * R_DEV + local).reshape(-1)
    return jnp.zeros((REQUEST_TOTAL,), jnp.int32).at[slot_index].set(request.astype(jnp.int32))


def draw_cache_length(key, part):
    first_key = jax.random.fold_in(key, 31)
    second_key = jax.random.fold_in(key, 32)
    third_key = jax.random.fold_in(key, 33)
    shifts = jax.random.randint(first_key, (REQUEST_TOTAL,), 0, 5)
    spans = jnp.right_shift(jnp.int32(CACHE_SLOTS), shifts.astype(jnp.int32))
    lengths = 1 + jax.random.randint(second_key, (REQUEST_TOTAL,), 0, spans)
    chosen = jax.random.randint(third_key, (), 0, REQUEST_TOTAL)
    return jnp.where(jnp.arange(REQUEST_TOTAL, dtype=jnp.int32) == chosen, CACHE_SLOTS, lengths).astype(jnp.int32)


def plant(array, own_key, smallest, top_value):
    longest = array.shape.index(max(array.shape))
    spots = []
    for shift in (0, 1):
        where = [jax.random.randint(jax.random.fold_in(own_key, axis), (), 0, length) for axis, length in enumerate(array.shape)]
        where[longest] = (where[longest] + shift) % array.shape[longest]
        spots.append(tuple(where))
    return array.at[spots[0]].set(smallest).at[spots[1]].set(top_value)


def steps_of(own_key, shape, cuts, least, high):
    gain, own = 1.0, jax.random.fold_in(own_key, 6)
    for dim, blocks in cuts:
        heights = jnp.exp(jax.random.uniform(jax.random.fold_in(own, dim), (blocks,), jnp.float32, least / len(cuts), high / len(cuts)))
        gain = gain * jnp.repeat(heights, shape[dim] // blocks).reshape([-1 if axis == dim else 1 for axis in range(len(shape))])
    return gain


def bell_draw(stream_key, shape, deviation, bound, pieces=(), held_as=jnp.bfloat16):
    factor_of = steps_of(stream_key, shape, pieces, -0.22, 0.18) if pieces else 1.0
    entries = jax.random.normal(stream_key, shape, jnp.float32) * deviation * factor_of
    return jnp.minimum(jnp.maximum(entries, -bound), bound).astype(held_as)


def setup_inputs(seed: int = 0) -> dict:
    key_list = jax.random.split(jax.random.key(seed), 10)
    return {
        "hidden": bell_draw(key_list[0], (REQUEST_TOTAL, VERIFIED_TOKENS, MODEL_WIDTH), 1.0, 6.0, ((0, 64), (2, 8))),
        "norm_gain": jnp.clip(1.0 + 0.18 * jax.random.normal(key_list[1], (MODEL_WIDTH,), jnp.float32), 0.099609375, 1.8984375).astype(jnp.bfloat16),
        "query_weight": bell_draw(key_list[2], (MODEL_WIDTH, HQ * HEAD_SIZE), MODEL_WIDTH ** -0.5, 0.125, ((1, 8),)),
        "key_value_matrix": bell_draw(key_list[3], (MODEL_WIDTH, KEY_VALUE_HEADS, 2 * HEAD_SIZE), MODEL_WIDTH ** -0.5, 0.125, ((1, 8),)),
        "output_weight": bell_draw(key_list[4], (HQ * HEAD_SIZE, MODEL_WIDTH), (HQ * HEAD_SIZE // 16) ** -0.5, 0.5, ((0, 8),)),
        "key_value_cache": draw_key_value_cache(jax.random.fold_in(key_list[9], 71), 0),
        "deal_order": draw_deal_order(jax.random.fold_in(key_list[9], 71), 0),
        "cache_length": draw_cache_length(jax.random.fold_in(key_list[9], 71), 0),
        "accepted": plant(jax.random.randint(key_list[8], (REQUEST_TOTAL,), 1, VERIFIED_TOKENS + 1), jax.random.fold_in(key_list[8], 1), 1, VERIFIED_TOKENS).astype(jnp.int32),
    }


masked_score = -1e+30

def rotate(values, positions):
    half_dim = HEAD_SIZE // 2
    frequency = 10000.0 ** (-2.0 * jnp.arange(half_dim, dtype=jnp.float32) / HEAD_SIZE)
    angles = positions.astype(jnp.float32)[..., None] * frequency
    cosine_part = jnp.cos(angles)
    sine_part = jnp.sin(angles)
    first_half = values[..., :half_dim]
    second_half = values[..., half_dim:]
    return jnp.concatenate([first_half * cosine_part - second_half * sine_part, second_half * cosine_part + first_half * sine_part], axis=-1)

def reference(hidden, norm_gain, query_weight, key_value_matrix, output_weight, key_value_cache, deal_order, cache_length, accepted):
    dealt = jnp.take(hidden, deal_order, axis=0)
    widened = dealt.astype(jnp.float32)
    variance = lax.optimization_barrier(jnp.mean(widened * widened, axis=-1, keepdims=True))
    normed = (widened * lax.rsqrt(variance + 1e-05) * norm_gain.astype(jnp.float32)).astype(jnp.bfloat16)
    positions = cache_length[:, None] + jnp.arange(VERIFIED_TOKENS, dtype=jnp.int32)[None, :]
    query_rows = jnp.einsum('rtd,de->rte', normed.astype(jnp.float32), query_weight.astype(jnp.float32))
    query_rows = query_rows.reshape(REQUEST_TOTAL, VERIFIED_TOKENS, KEY_VALUE_HEADS, HEADS_PER_GROUP, HEAD_SIZE)
    query_rows = rotate(query_rows, positions[:, :, None, None]).astype(jnp.bfloat16)
    projected = jnp.einsum('rtd,dge->rtge', normed.astype(jnp.float32), key_value_matrix.astype(jnp.float32))
    fresh = jnp.concatenate([rotate(projected[..., :HEAD_SIZE], positions[:, :, None]), projected[..., HEAD_SIZE:]], axis=-1).astype(jnp.bfloat16)
    keep = (jnp.arange(VERIFIED_TOKENS, dtype=jnp.int32)[None, :] < accepted[:, None])[:, :, None, None]
    new_entries = jnp.where(keep, fresh, jnp.zeros_like(fresh))
    all_keys = jnp.concatenate([key_value_cache[..., :HEAD_SIZE], fresh[..., :HEAD_SIZE]], axis=1).astype(jnp.float32)
    all_values = jnp.concatenate([key_value_cache[..., HEAD_SIZE:], fresh[..., HEAD_SIZE:]], axis=1).astype(jnp.float32)
    scores = jnp.einsum('rtghd,rcgd->rghtc', query_rows.astype(jnp.float32), all_keys) * (1.0 / jnp.sqrt(jnp.float32(HEAD_SIZE)))
    cache_visible = jnp.arange(CACHE_SLOTS, dtype=jnp.int32)[None, :] < cache_length[:, None]
    cache_visible = jnp.broadcast_to(cache_visible[:, None, :], (REQUEST_TOTAL, VERIFIED_TOKENS, CACHE_SLOTS))
    causal = jnp.arange(VERIFIED_TOKENS, dtype=jnp.int32)[:, None] >= jnp.arange(VERIFIED_TOKENS, dtype=jnp.int32)[None, :]
    causal = jnp.broadcast_to(causal[None, :, :], (REQUEST_TOTAL, VERIFIED_TOKENS, VERIFIED_TOKENS))
    visible = jnp.concatenate([cache_visible, causal], axis=2)[:, None, None, :, :]
    scores = jnp.where(visible, scores, masked_score)
    largest = lax.optimization_barrier(jnp.max(scores, axis=-1, keepdims=True))
    expos = jnp.exp(scores - largest)
    weights = (expos / lax.optimization_barrier(jnp.sum(expos, axis=-1, keepdims=True))).astype(jnp.bfloat16)
    mixed = jnp.einsum('rghtc,rcgd->rtghd', weights.astype(jnp.float32), all_values).astype(jnp.bfloat16)
    mixed = mixed.reshape(REQUEST_TOTAL, VERIFIED_TOKENS, HQ * HEAD_SIZE)
    out_dealt = jnp.einsum('rte,ed->rtd', mixed.astype(jnp.float32), output_weight.astype(jnp.float32)).astype(jnp.bfloat16)
    block_output = jnp.zeros_like(out_dealt).at[deal_order].set(out_dealt)
    return (block_output, new_entries)
```

```python
import functools
import math

import jax
import jax.numpy as jnp
from jax import lax
from jax.sharding import PartitionSpec as P

HEAD_SIZE = 80


masked_score = -1e30


def rotate(values, positions):
    half_dim = HEAD_SIZE // 2
    frequency = 10000.0 ** (-2.0 * jnp.arange(half_dim, dtype=jnp.float32) / HEAD_SIZE)
    angles = positions.astype(jnp.float32)[..., None] * frequency
    cosine_part = jnp.cos(angles)
    sine_part = jnp.sin(angles)
    first_half = values[..., :half_dim]
    second_half = values[..., half_dim:]
    return jnp.concatenate(
        [
            first_half * cosine_part - second_half * sine_part,
            second_half * cosine_part + first_half * sine_part,
        ],
        axis=-1,
    )


def attend(query_rows, key_value_cache, fresh, cache_length):
    scale = 1.0 / math.sqrt(HEAD_SIZE)
    slot_count = query_rows.shape[0]
    verified = query_rows.shape[1]
    cache_keys = key_value_cache[..., :HEAD_SIZE]
    cache_values = key_value_cache[..., HEAD_SIZE:]
    fresh_keys = fresh[..., :HEAD_SIZE]
    fresh_values = fresh[..., HEAD_SIZE:]
    cache_scores = (
        jnp.einsum("rtghd,rcgd->rghtc", query_rows, cache_keys, preferred_element_type=jnp.float32)
        * scale
    )
    visible = jnp.arange(key_value_cache.shape[1], dtype=jnp.int32)[None, :] < cache_length[:, None]
    cache_scores = jnp.where(visible[:, None, None, None, :], cache_scores, masked_score)
    fresh_scores = (
        jnp.einsum("rtghd,rugd->rghtu", query_rows, fresh_keys, preferred_element_type=jnp.float32)
        * scale
    )
    causal = (
        jnp.arange(verified, dtype=jnp.int32)[:, None]
        >= jnp.arange(verified, dtype=jnp.int32)[None, :]
    )
    fresh_scores = jnp.where(causal[None, None, None, :, :], fresh_scores, masked_score)
    largest = jnp.maximum(jnp.max(cache_scores, axis=-1), jnp.max(fresh_scores, axis=-1))[..., None]
    cache_expos = jnp.exp(cache_scores - largest)
    fresh_expos = jnp.exp(fresh_scores - largest)
    totals = jnp.sum(cache_expos, axis=-1, keepdims=True) + jnp.sum(
        fresh_expos, axis=-1, keepdims=True
    )
    cache_weights = (cache_expos / totals).astype(jnp.bfloat16)
    fresh_weights = (fresh_expos / totals).astype(jnp.bfloat16)
    mixed = jnp.einsum(
        "rghtc,rcgd->rtghd", cache_weights, cache_values, preferred_element_type=jnp.float32
    )
    mixed = mixed + jnp.einsum(
        "rghtu,rugd->rtghd", fresh_weights, fresh_values, preferred_element_type=jnp.float32
    )
    return mixed.astype(jnp.bfloat16).reshape(slot_count, verified, -1)


def body(
    hidden,
    norm_gain,
    query_weight,
    key_value_matrix,
    output_weight,
    key_value_cache,
    deal_order,
    cache_length,
    accepted,
    *,
    peers,
    shards,
):
    slot_count = deal_order.shape[0]
    verified = hidden.shape[1]
    width = hidden.shape[2]
    source = deal_order // slot_count
    local = deal_order % slot_count
    match = source[None, :] == jnp.arange(peers, dtype=jnp.int32)[:, None]
    wish = jnp.sum(jnp.where(match, local[None, :] + 1, 0), axis=1) - 1
    wanted = lax.all_to_all(wish, "req", 0, 0, tiled=True)
    pick = (wanted[:, None] == jnp.arange(slot_count, dtype=jnp.int32)[None, :]).astype(jnp.bfloat16)
    outgoing = jnp.einsum(
        "dj,jtf->dtf", pick, hidden, preferred_element_type=jnp.float32
    ).astype(jnp.bfloat16)
    incoming = lax.all_to_all(outgoing, "req", 0, 0, tiled=True)
    take = match.astype(jnp.bfloat16)
    dealt_rows = jnp.einsum(
        "pi,ptf->itf", take, incoming, preferred_element_type=jnp.float32
    ).astype(jnp.bfloat16)
    rows = slot_count * verified
    features = lax.all_gather(dealt_rows.reshape(rows, width), "tp", axis=0, tiled=False)
    widened = features.astype(jnp.float32)
    variance = jnp.mean(widened * widened, axis=(0, 2), keepdims=True)
    gain = norm_gain.reshape(shards, 1, width).astype(jnp.float32)
    normed = (widened * lax.rsqrt(variance + 1e-05) * gain).astype(jnp.bfloat16)
    heads_here = query_weight.shape[1] // HEAD_SIZE
    groups_here = key_value_matrix.shape[1]
    positions = cache_length[:, None] + jnp.arange(verified, dtype=jnp.int32)[None, :]
    query_rows = jnp.einsum(
        "knf,kfe->ne",
        normed,
        query_weight.reshape(shards, width, -1),
        preferred_element_type=jnp.float32,
    )
    query_rows = query_rows.reshape(
        slot_count, verified, groups_here, heads_here // groups_here, HEAD_SIZE
    )
    query_rows = rotate(query_rows, positions[:, :, None, None]).astype(jnp.bfloat16)
    projected = jnp.einsum(
        "knf,kfge->nge",
        normed,
        key_value_matrix.reshape(shards, width, groups_here, -1),
        preferred_element_type=jnp.float32,
    ).reshape(slot_count, verified, groups_here, -1)
    fresh = jnp.concatenate(
        [rotate(projected[..., :HEAD_SIZE], positions[:, :, None]), projected[..., HEAD_SIZE:]],
        axis=-1,
    ).astype(jnp.bfloat16)
    keep = (jnp.arange(verified, dtype=jnp.int32)[None, :] < accepted[:, None])[:, :, None, None]
    new_entries = jnp.where(keep, fresh, jnp.zeros_like(fresh))
    mixed = attend(query_rows, key_value_cache, fresh, cache_length)
    partial_sum = jnp.einsum(
        "ne,ekf->knf",
        mixed.reshape(rows, -1),
        output_weight.reshape(-1, shards, width),
        preferred_element_type=jnp.float32,
    )
    out_dealt = lax.psum_scatter(partial_sum, "tp", scatter_dimension=0, tiled=True)
    out_dealt = out_dealt.reshape(slot_count, verified, width).astype(jnp.bfloat16)
    back_out = jnp.einsum(
        "pi,itf->ptf", take, out_dealt, preferred_element_type=jnp.float32
    ).astype(jnp.bfloat16)
    returned = lax.all_to_all(back_out, "req", 0, 0, tiled=True)
    block_output = jnp.einsum(
        "dj,dtf->jtf", pick, returned, preferred_element_type=jnp.float32
    ).astype(jnp.bfloat16)
    return (block_output, new_entries)


def solution(mesh):
    placed = (
        P("req", None, "tp"),
        P(),
        P(None, "tp"),
        P(None, "tp", None),
        P("tp", None),
        P("req", None, "tp", None),
        P("req"),
        P("req"),
        P("req"),
    )
    return jax.shard_map(
        functools.partial(body, peers=mesh.shape["req"], shards=mesh.shape["tp"]),
        mesh=mesh,
        in_specs=placed,
        out_specs=(P("req", None, "tp"), P("req", None, "tp", None)),
        check_vma=False,
    )
```

```python
import functools
import math

import jax
import jax.numpy as jnp
from jax import lax
from jax.sharding import PartitionSpec as P

HEAD_SIZE = 80


masked_score = -1e30


def rotate(values, positions):
    half_dim = HEAD_SIZE // 2
    frequency = 10000.0 ** (-2.0 * jnp.arange(half_dim, dtype=jnp.float32) / HEAD_SIZE)
    angles = positions.astype(jnp.float32)[..., None] * frequency
    cosine_part = jnp.cos(angles)
    sine_part = jnp.sin(angles)
    first_half = values[..., :half_dim]
    second_half = values[..., half_dim:]
    return jnp.concatenate(
        [
            first_half * cosine_part - second_half * sine_part,
            second_half * cosine_part + first_half * sine_part,
        ],
        axis=-1,
    )


def attend(query_rows, key_value_cache, fresh, cache_length):
    scale = 1.0 / math.sqrt(HEAD_SIZE)
    slot_count = query_rows.shape[0]
    verified = query_rows.shape[1]
    cache_keys = key_value_cache[..., :HEAD_SIZE]
    cache_values = key_value_cache[..., HEAD_SIZE:]
    fresh_keys = fresh[..., :HEAD_SIZE]
    fresh_values = fresh[..., HEAD_SIZE:]
    cache_scores = (
        jnp.einsum("rtghd,rcgd->rghtc", query_rows, cache_keys, preferred_element_type=jnp.float32)
        * scale
    )
    visible = jnp.arange(key_value_cache.shape[1], dtype=jnp.int32)[None, :] < cache_length[:, None]
    cache_scores = jnp.where(visible[:, None, None, None, :], cache_scores, masked_score)
    fresh_scores = (
        jnp.einsum("rtghd,rugd->rghtu", query_rows, fresh_keys, preferred_element_type=jnp.float32)
        * scale
    )
    causal = (
        jnp.arange(verified, dtype=jnp.int32)[:, None]
        >= jnp.arange(verified, dtype=jnp.int32)[None, :]
    )
    fresh_scores = jnp.where(causal[None, None, None, :, :], fresh_scores, masked_score)
    largest = jnp.maximum(jnp.max(cache_scores, axis=-1), jnp.max(fresh_scores, axis=-1))[..., None]
    cache_expos = jnp.exp(cache_scores - largest)
    fresh_expos = jnp.exp(fresh_scores - largest)
    totals = jnp.sum(cache_expos, axis=-1, keepdims=True) + jnp.sum(
        fresh_expos, axis=-1, keepdims=True
    )
    cache_weights = (cache_expos / totals).astype(jnp.bfloat16)
    fresh_weights = (fresh_expos / totals).astype(jnp.bfloat16)
    mixed = jnp.einsum(
        "rghtc,rcgd->rtghd", cache_weights, cache_values, preferred_element_type=jnp.float32
    )
    mixed = mixed + jnp.einsum(
        "rghtu,rugd->rtghd", fresh_weights, fresh_values, preferred_element_type=jnp.float32
    )
    return mixed.astype(jnp.bfloat16).reshape(slot_count, verified, -1)


def body(
    hidden,
    norm_gain,
    query_weight,
    key_value_matrix,
    output_weight,
    key_value_cache,
    deal_order,
    cache_length,
    accepted,
    *,
    peers,
    shards,
):
    slot_count = deal_order.shape[0]
    verified = hidden.shape[1]
    width = hidden.shape[2]
    source = deal_order // slot_count
    local = deal_order % slot_count
    match = source[None, :] == jnp.arange(peers, dtype=jnp.int32)[:, None]
    wish = jnp.sum(jnp.where(match, local[None, :] + 1, 0), axis=1) - 1
    wanted = lax.all_to_all(wish, "req", 0, 0, tiled=True)
    pick = (wanted[:, None] == jnp.arange(slot_count, dtype=jnp.int32)[None, :]).astype(jnp.bfloat16)
    outgoing = jnp.einsum(
        "dj,jtf->dtf", pick, hidden, preferred_element_type=jnp.float32
    ).astype(jnp.bfloat16)
    incoming = lax.all_to_all(outgoing, "req", 0, 0, tiled=True)
    take = match.astype(jnp.bfloat16)
    dealt_rows = jnp.einsum(
        "pi,ptf->itf", take, incoming, preferred_element_type=jnp.float32
    ).astype(jnp.bfloat16)
    rows = slot_count * verified
    features = lax.all_gather(dealt_rows.reshape(rows, width), "tp", axis=0, tiled=False)
    widened = features.astype(jnp.float32)
    variance = jnp.mean(widened * widened, axis=(0, 2), keepdims=True)
    gain = norm_gain.reshape(shards, 1, width).astype(jnp.float32)
    normed = (widened * lax.rsqrt(variance + 1e-05) * gain).astype(jnp.bfloat16)
    heads_here = query_weight.shape[1] // HEAD_SIZE
    groups_here = key_value_matrix.shape[1]
    positions = cache_length[:, None] + jnp.arange(verified, dtype=jnp.int32)[None, :]
    query_rows = jnp.einsum(
        "knf,kfe->ne",
        normed,
        query_weight.reshape(shards, width, -1),
        preferred_element_type=jnp.float32,
    )
    query_rows = query_rows.reshape(
        slot_count, verified, groups_here, heads_here // groups_here, HEAD_SIZE
    )
    query_rows = rotate(query_rows, positions[:, :, None, None]).astype(jnp.bfloat16)
    projected = jnp.einsum(
        "knf,kfge->nge",
        normed,
        key_value_matrix.reshape(shards, width, groups_here, -1),
        preferred_element_type=jnp.float32,
    ).reshape(slot_count, verified, groups_here, -1)
    fresh = jnp.concatenate(
        [rotate(projected[..., :HEAD_SIZE], positions[:, :, None]), projected[..., HEAD_SIZE:]],
        axis=-1,
    ).astype(jnp.bfloat16)
    keep = (jnp.arange(verified, dtype=jnp.int32)[None, :] < accepted[:, None])[:, :, None, None]
    new_entries = jnp.where(keep, fresh, jnp.zeros_like(fresh))
    mixed = attend(query_rows, key_value_cache, fresh, cache_length)
    partial_sum = jnp.einsum(
        "ne,ekf->knf",
        mixed.reshape(rows, -1),
        output_weight.reshape(-1, shards, width),
        preferred_element_type=jnp.float32,
    )
    pieces = lax.all_to_all(partial_sum.astype(jnp.bfloat16), "tp", 0, 0, tiled=True)
    out_dealt = jnp.sum(pieces.astype(jnp.float32), axis=0)
    out_dealt = out_dealt.reshape(slot_count, verified, width).astype(jnp.bfloat16)
    back_out = jnp.einsum(
        "pi,itf->ptf", take, out_dealt, preferred_element_type=jnp.float32
    ).astype(jnp.bfloat16)
    returned = lax.all_to_all(back_out, "req", 0, 0, tiled=True)
    block_output = jnp.einsum(
        "dj,dtf->jtf", pick, returned, preferred_element_type=jnp.float32
    ).astype(jnp.bfloat16)
    return (block_output, new_entries)


def solution(mesh):
    placed = (
        P("req", None, "tp"),
        P(),
        P(None, "tp"),
        P(None, "tp", None),
        P("tp", None),
        P("req", None, "tp", None),
        P("req"),
        P("req"),
        P("req"),
    )
    return jax.shard_map(
        functools.partial(body, peers=mesh.shape["req"], shards=mesh.shape["tp"]),
        mesh=mesh,
        in_specs=placed,
        out_specs=(P("req", None, "tp"), P("req", None, "tp", None)),
        check_vma=False,
    )
```

```python
import functools
import math

import jax
import jax.numpy as jnp
from jax import lax
from jax.sharding import PartitionSpec as P

HEAD_SIZE = 80


masked_score = -1e30


def rotate(values, positions):
    half_dim = HEAD_SIZE // 2
    frequency = 10000.0 ** (-2.0 * jnp.arange(half_dim, dtype=jnp.float32) / HEAD_SIZE)
    angles = positions.astype(jnp.float32)[..., None] * frequency
    cosine_part = jnp.cos(angles)
    sine_part = jnp.sin(angles)
    first_half = values[..., :half_dim]
    second_half = values[..., half_dim:]
    return jnp.concatenate(
        [
            first_half * cosine_part - second_half * sine_part,
            second_half * cosine_part + first_half * sine_part,
        ],
        axis=-1,
    )


def attend(query_rows, key_value_cache, fresh, cache_length):
    scale = 1.0 / math.sqrt(HEAD_SIZE)
    slot_count = query_rows.shape[0]
    verified = query_rows.shape[1]
    cache_keys = key_value_cache[..., :HEAD_SIZE]
    cache_values = key_value_cache[..., HEAD_SIZE:]
    fresh_keys = fresh[..., :HEAD_SIZE]
    fresh_values = fresh[..., HEAD_SIZE:]
    cache_scores = (
        jnp.einsum("rtghd,rcgd->rghtc", query_rows, cache_keys, preferred_element_type=jnp.float32)
        * scale
    )
    visible = jnp.arange(key_value_cache.shape[1], dtype=jnp.int32)[None, :] < cache_length[:, None]
    cache_scores = jnp.where(visible[:, None, None, None, :], cache_scores, masked_score)
    fresh_scores = (
        jnp.einsum("rtghd,rugd->rghtu", query_rows, fresh_keys, preferred_element_type=jnp.float32)
        * scale
    )
    causal = (
        jnp.arange(verified, dtype=jnp.int32)[:, None]
        >= jnp.arange(verified, dtype=jnp.int32)[None, :]
    )
    fresh_scores = jnp.where(causal[None, None, None, :, :], fresh_scores, masked_score)
    largest = jnp.maximum(jnp.max(cache_scores, axis=-1), jnp.max(fresh_scores, axis=-1))[..., None]
    cache_expos = jnp.exp(cache_scores - largest)
    fresh_expos = jnp.exp(fresh_scores - largest)
    totals = jnp.sum(cache_expos, axis=-1, keepdims=True) + jnp.sum(
        fresh_expos, axis=-1, keepdims=True
    )
    cache_weights = (cache_expos / totals).astype(jnp.bfloat16)
    fresh_weights = (fresh_expos / totals).astype(jnp.bfloat16)
    mixed = jnp.einsum(
        "rghtc,rcgd->rtghd", cache_weights, cache_values, preferred_element_type=jnp.float32
    )
    mixed = mixed + jnp.einsum(
        "rghtu,rugd->rtghd", fresh_weights, fresh_values, preferred_element_type=jnp.float32
    )
    return mixed.astype(jnp.bfloat16).reshape(slot_count, verified, -1)


def body(
    hidden,
    norm_gain,
    query_weight,
    key_value_matrix,
    output_weight,
    key_value_cache,
    deal_order,
    cache_length,
    accepted,
    *,
    peers,
    shards,
):
    slot_count = deal_order.shape[0]
    verified = hidden.shape[1]
    width = hidden.shape[2]
    source = deal_order // slot_count
    local = deal_order % slot_count
    match = source[None, :] == jnp.arange(peers, dtype=jnp.int32)[:, None]
    wish = jnp.sum(jnp.where(match, local[None, :] + 1, 0), axis=1) - 1
    wanted = lax.all_to_all(wish, "req", 0, 0, tiled=True)
    pick = (wanted[:, None] == jnp.arange(slot_count, dtype=jnp.int32)[None, :]).astype(jnp.bfloat16)
    row_size = verified * width
    tile = 16 * 128
    padded = -(-row_size // tile) * tile
    outgoing = jnp.einsum(
        "dj,jx->dx", pick, hidden.reshape(slot_count, row_size), preferred_element_type=jnp.float32
    ).astype(jnp.bfloat16)
    outgoing = jnp.pad(outgoing, ((0, 0), (0, padded - row_size))).reshape(peers, padded // 128, 128)
    incoming = lax.all_to_all(outgoing, "req", 0, 0, tiled=True)
    incoming = incoming.reshape(peers, padded)[:, :row_size]
    take = match.astype(jnp.bfloat16)
    dealt_rows = jnp.einsum(
        "pi,px->ix", take, incoming, preferred_element_type=jnp.float32
    ).astype(jnp.bfloat16)
    rows = slot_count * verified
    features = lax.all_gather(dealt_rows.reshape(rows, width), "tp", axis=0, tiled=False)
    widened = features.astype(jnp.float32)
    variance = jnp.mean(widened * widened, axis=(0, 2), keepdims=True)
    gain = norm_gain.reshape(shards, 1, width).astype(jnp.float32)
    normed = (widened * lax.rsqrt(variance + 1e-05) * gain).astype(jnp.bfloat16)
    heads_here = query_weight.shape[1] // HEAD_SIZE
    groups_here = key_value_matrix.shape[1]
    positions = cache_length[:, None] + jnp.arange(verified, dtype=jnp.int32)[None, :]
    query_rows = jnp.einsum(
        "knf,kfe->ne",
        normed,
        query_weight.reshape(shards, width, -1),
        preferred_element_type=jnp.float32,
    )
    query_rows = query_rows.reshape(
        slot_count, verified, groups_here, heads_here // groups_here, HEAD_SIZE
    )
    query_rows = rotate(query_rows, positions[:, :, None, None]).astype(jnp.bfloat16)
    projected = jnp.einsum(
        "knf,kfge->nge",
        normed,
        key_value_matrix.reshape(shards, width, groups_here, -1),
        preferred_element_type=jnp.float32,
    ).reshape(slot_count, verified, groups_here, -1)
    fresh = jnp.concatenate(
        [rotate(projected[..., :HEAD_SIZE], positions[:, :, None]), projected[..., HEAD_SIZE:]],
        axis=-1,
    ).astype(jnp.bfloat16)
    keep = (jnp.arange(verified, dtype=jnp.int32)[None, :] < accepted[:, None])[:, :, None, None]
    new_entries = jnp.where(keep, fresh, jnp.zeros_like(fresh))
    mixed = attend(query_rows, key_value_cache, fresh, cache_length)
    partial_sum = jnp.einsum(
        "ne,ekf->knf",
        mixed.reshape(rows, -1),
        output_weight.reshape(-1, shards, width),
        preferred_element_type=jnp.float32,
    )
    pieces = lax.all_to_all(partial_sum.astype(jnp.bfloat16), "tp", 0, 0, tiled=True)
    out_dealt = jnp.sum(pieces.astype(jnp.float32), axis=0)
    out_dealt = out_dealt.reshape(slot_count, verified, width).astype(jnp.bfloat16)
    back_out = jnp.einsum(
        "pi,ix->px", take, out_dealt.reshape(slot_count, row_size), preferred_element_type=jnp.float32
    ).astype(jnp.bfloat16)
    back_out = jnp.pad(back_out, ((0, 0), (0, padded - row_size))).reshape(peers, padded // 128, 128)
    returned = lax.all_to_all(back_out, "req", 0, 0, tiled=True)
    returned = returned.reshape(peers, padded)[:, :row_size]
    block_output = jnp.einsum(
        "dj,dx->jx", pick, returned, preferred_element_type=jnp.float32
    ).astype(jnp.bfloat16).reshape(slot_count, verified, width)
    return (block_output, new_entries)


def solution(mesh):
    placed = (
        P("req", None, "tp"),
        P(),
        P(None, "tp"),
        P(None, "tp", None),
        P("tp", None),
        P("req", None, "tp", None),
        P("req"),
        P("req"),
        P("req"),
    )
    return jax.shard_map(
        functools.partial(body, peers=mesh.shape["req"], shards=mesh.shape["tp"]),
        mesh=mesh,
        in_specs=placed,
        out_specs=(P("req", None, "tp"), P("req", None, "tp", None)),
        check_vma=False,
    )
```

```python
import functools
import math

import jax
import jax.numpy as jnp
from jax import lax
from jax.sharding import PartitionSpec as P

HEAD_SIZE = 80


masked_score = -1e30


def rotate(values, positions):
    half_dim = HEAD_SIZE // 2
    frequency = 10000.0 ** (-2.0 * jnp.arange(half_dim, dtype=jnp.float32) / HEAD_SIZE)
    angles = positions.astype(jnp.float32)[..., None] * frequency
    cosine_part = jnp.cos(angles)
    sine_part = jnp.sin(angles)
    first_half = values[..., :half_dim]
    second_half = values[..., half_dim:]
    return jnp.concatenate(
        [
            first_half * cosine_part - second_half * sine_part,
            second_half * cosine_part + first_half * sine_part,
        ],
        axis=-1,
    )


def attend(query_rows, key_value_cache, fresh, cache_length):
    scale = 1.0 / math.sqrt(HEAD_SIZE)
    slot_count = query_rows.shape[0]
    verified = query_rows.shape[1]
    cache_keys = key_value_cache[..., :HEAD_SIZE]
    cache_values = key_value_cache[..., HEAD_SIZE:]
    fresh_keys = fresh[..., :HEAD_SIZE]
    fresh_values = fresh[..., HEAD_SIZE:]
    cache_scores = (
        jnp.einsum("rtghd,rcgd->rghtc", query_rows, cache_keys, preferred_element_type=jnp.float32)
        * scale
    )
    visible = jnp.arange(key_value_cache.shape[1], dtype=jnp.int32)[None, :] < cache_length[:, None]
    cache_scores = jnp.where(visible[:, None, None, None, :], cache_scores, masked_score)
    fresh_scores = (
        jnp.einsum("rtghd,rugd->rghtu", query_rows, fresh_keys, preferred_element_type=jnp.float32)
        * scale
    )
    causal = (
        jnp.arange(verified, dtype=jnp.int32)[:, None]
        >= jnp.arange(verified, dtype=jnp.int32)[None, :]
    )
    fresh_scores = jnp.where(causal[None, None, None, :, :], fresh_scores, masked_score)
    largest = jnp.maximum(jnp.max(cache_scores, axis=-1), jnp.max(fresh_scores, axis=-1))[..., None]
    cache_expos = jnp.exp(cache_scores - largest)
    fresh_expos = jnp.exp(fresh_scores - largest)
    totals = jnp.sum(cache_expos, axis=-1, keepdims=True) + jnp.sum(
        fresh_expos, axis=-1, keepdims=True
    )
    cache_weights = (cache_expos / totals).astype(jnp.bfloat16)
    fresh_weights = (fresh_expos / totals).astype(jnp.bfloat16)
    mixed = jnp.einsum(
        "rghtc,rcgd->rtghd", cache_weights, cache_values, preferred_element_type=jnp.float32
    )
    mixed = mixed + jnp.einsum(
        "rghtu,rugd->rtghd", fresh_weights, fresh_values, preferred_element_type=jnp.float32
    )
    return mixed.astype(jnp.bfloat16).reshape(slot_count, verified, -1)


def body(
    hidden,
    norm_gain,
    query_weight,
    key_value_matrix,
    output_weight,
    key_value_cache,
    deal_order,
    cache_length,
    accepted,
    *,
    peers,
    shards,
):
    slot_count = deal_order.shape[0]
    verified = hidden.shape[1]
    width = hidden.shape[2]
    source = deal_order // slot_count
    local = deal_order % slot_count
    match = source[None, :] == jnp.arange(peers, dtype=jnp.int32)[:, None]
    wish = jnp.sum(jnp.where(match, local[None, :] + 1, 0), axis=1) - 1
    wanted = lax.all_to_all(wish, "req", 0, 0, tiled=True)
    pick = (wanted[:, None] == jnp.arange(slot_count, dtype=jnp.int32)[None, :]).astype(jnp.bfloat16)
    row_size = verified * width
    tile = 16 * 128
    padded = -(-row_size // tile) * tile
    outgoing = jnp.einsum(
        "dj,jx->dx", pick, hidden.reshape(slot_count, row_size), preferred_element_type=jnp.float32
    ).astype(jnp.bfloat16)
    outgoing = jnp.pad(outgoing, ((0, 0), (0, padded - row_size))).reshape(peers, padded // 128, 128)
    incoming = lax.all_to_all(outgoing, "req", 0, 0, tiled=True)
    incoming = incoming.reshape(peers, padded)[:, :row_size]
    take = match.astype(jnp.bfloat16)
    dealt_rows = jnp.einsum(
        "pi,px->ix", take, incoming, preferred_element_type=jnp.float32
    ).astype(jnp.bfloat16)
    rows = slot_count * verified
    lanes = rows * width // 128
    features = lax.all_gather(dealt_rows.reshape(lanes, 128), "tp", axis=0, tiled=False)
    features = features.reshape(shards, rows, width)
    widened = features.astype(jnp.float32)
    variance = jnp.mean(widened * widened, axis=(0, 2), keepdims=True)
    gain = norm_gain.reshape(shards, 1, width).astype(jnp.float32)
    normed = (widened * lax.rsqrt(variance + 1e-05) * gain).astype(jnp.bfloat16)
    heads_here = query_weight.shape[1] // HEAD_SIZE
    groups_here = key_value_matrix.shape[1]
    positions = cache_length[:, None] + jnp.arange(verified, dtype=jnp.int32)[None, :]
    query_rows = jnp.einsum(
        "knf,kfe->ne",
        normed,
        query_weight.reshape(shards, width, -1),
        preferred_element_type=jnp.float32,
    )
    query_rows = query_rows.reshape(
        slot_count, verified, groups_here, heads_here // groups_here, HEAD_SIZE
    )
    query_rows = rotate(query_rows, positions[:, :, None, None]).astype(jnp.bfloat16)
    projected = jnp.einsum(
        "knf,kfge->nge",
        normed,
        key_value_matrix.reshape(shards, width, groups_here, -1),
        preferred_element_type=jnp.float32,
    ).reshape(slot_count, verified, groups_here, -1)
    fresh = jnp.concatenate(
        [rotate(projected[..., :HEAD_SIZE], positions[:, :, None]), projected[..., HEAD_SIZE:]],
        axis=-1,
    ).astype(jnp.bfloat16)
    keep = (jnp.arange(verified, dtype=jnp.int32)[None, :] < accepted[:, None])[:, :, None, None]
    new_entries = jnp.where(keep, fresh, jnp.zeros_like(fresh))
    mixed = attend(query_rows, key_value_cache, fresh, cache_length)
    partial_sum = jnp.einsum(
        "ne,ekf->knf",
        mixed.reshape(rows, -1),
        output_weight.reshape(-1, shards, width),
        preferred_element_type=jnp.float32,
    )
    pieces = partial_sum.astype(jnp.bfloat16).reshape(shards, lanes, 128)
    pieces = lax.all_to_all(pieces, "tp", 0, 0, tiled=True)
    out_dealt = jnp.sum(pieces.astype(jnp.float32), axis=0)
    out_dealt = out_dealt.reshape(slot_count, verified, width).astype(jnp.bfloat16)
    back_out = jnp.einsum(
        "pi,ix->px", take, out_dealt.reshape(slot_count, row_size), preferred_element_type=jnp.float32
    ).astype(jnp.bfloat16)
    back_out = jnp.pad(back_out, ((0, 0), (0, padded - row_size))).reshape(peers, padded // 128, 128)
    returned = lax.all_to_all(back_out, "req", 0, 0, tiled=True)
    returned = returned.reshape(peers, padded)[:, :row_size]
    block_output = jnp.einsum(
        "dj,dx->jx", pick, returned, preferred_element_type=jnp.float32
    ).astype(jnp.bfloat16).reshape(slot_count, verified, width)
    return (block_output, new_entries)


def solution(mesh):
    placed = (
        P("req", None, "tp"),
        P(),
        P(None, "tp"),
        P(None, "tp", None),
        P("tp", None),
        P("req", None, "tp", None),
        P("req"),
        P("req"),
        P("req"),
    )
    return jax.shard_map(
        functools.partial(body, peers=mesh.shape["req"], shards=mesh.shape["tp"]),
        mesh=mesh,
        in_specs=placed,
        out_specs=(P("req", None, "tp"), P("req", None, "tp", None)),
        check_vma=False,
    )
```

```python
import functools
import math

import jax
import jax.numpy as jnp
from jax import lax
from jax.sharding import PartitionSpec as P

HEAD_SIZE = 80


masked_score = -1e30


def rotate(values, positions):
    half_dim = HEAD_SIZE // 2
    frequency = 10000.0 ** (-2.0 * jnp.arange(half_dim, dtype=jnp.float32) / HEAD_SIZE)
    angles = positions.astype(jnp.float32)[..., None] * frequency
    cosine_part = jnp.cos(angles)
    sine_part = jnp.sin(angles)
    first_half = values[..., :half_dim]
    second_half = values[..., half_dim:]
    return jnp.concatenate(
        [
            first_half * cosine_part - second_half * sine_part,
            second_half * cosine_part + first_half * sine_part,
        ],
        axis=-1,
    )


def attend(query_rows, key_value_cache, fresh, cache_length):
    scale = 1.0 / math.sqrt(HEAD_SIZE)
    slot_count = query_rows.shape[0]
    verified = query_rows.shape[1]
    cache_keys = key_value_cache[..., :HEAD_SIZE]
    cache_values = key_value_cache[..., HEAD_SIZE:]
    fresh_keys = fresh[..., :HEAD_SIZE]
    fresh_values = fresh[..., HEAD_SIZE:]
    cache_scores = (
        jnp.einsum("rtghd,rcgd->rghtc", query_rows, cache_keys, preferred_element_type=jnp.float32)
        * scale
    )
    visible = jnp.arange(key_value_cache.shape[1], dtype=jnp.int32)[None, :] < cache_length[:, None]
    cache_scores = jnp.where(visible[:, None, None, None, :], cache_scores, masked_score)
    fresh_scores = (
        jnp.einsum("rtghd,rugd->rghtu", query_rows, fresh_keys, preferred_element_type=jnp.float32)
        * scale
    )
    causal = (
        jnp.arange(verified, dtype=jnp.int32)[:, None]
        >= jnp.arange(verified, dtype=jnp.int32)[None, :]
    )
    fresh_scores = jnp.where(causal[None, None, None, :, :], fresh_scores, masked_score)
    largest = jnp.maximum(jnp.max(cache_scores, axis=-1), jnp.max(fresh_scores, axis=-1))[..., None]
    cache_expos = jnp.exp(cache_scores - largest)
    fresh_expos = jnp.exp(fresh_scores - largest)
    totals = jnp.sum(cache_expos, axis=-1, keepdims=True) + jnp.sum(
        fresh_expos, axis=-1, keepdims=True
    )
    cache_weights = (cache_expos / totals).astype(jnp.bfloat16)
    fresh_weights = (fresh_expos / totals).astype(jnp.bfloat16)
    mixed = jnp.einsum(
        "rghtc,rcgd->rtghd", cache_weights, cache_values, preferred_element_type=jnp.float32
    )
    mixed = mixed + jnp.einsum(
        "rghtu,rugd->rtghd", fresh_weights, fresh_values, preferred_element_type=jnp.float32
    )
    return mixed.astype(jnp.bfloat16).reshape(slot_count, verified, -1)


def body(
    hidden,
    norm_gain,
    query_weight,
    key_value_matrix,
    output_weight,
    key_value_cache,
    deal_order,
    cache_length,
    accepted,
    *,
    peers,
    shards,
):
    slot_count = deal_order.shape[0]
    verified = hidden.shape[1]
    width = hidden.shape[2]
    source = deal_order // slot_count
    local = deal_order % slot_count
    match = source[None, :] == jnp.arange(peers, dtype=jnp.int32)[:, None]
    wish = jnp.sum(jnp.where(match, local[None, :] + 1, 0), axis=1) - 1
    wanted = lax.all_to_all(wish, "req", 0, 0, tiled=True)
    pick = (wanted[:, None] == jnp.arange(slot_count, dtype=jnp.int32)[None, :]).astype(jnp.bfloat16)
    row_size = verified * width
    tile = 16 * 128
    padded = -(-row_size // tile) * tile
    outgoing = jnp.einsum(
        "dj,jx->dx", pick, hidden.reshape(slot_count, row_size), preferred_element_type=jnp.float32
    ).astype(jnp.bfloat16)
    outgoing = jnp.pad(outgoing, ((0, 0), (0, padded - row_size))).reshape(peers, padded // 128, 128)
    incoming = lax.all_to_all(outgoing, "req", 0, 0, tiled=True)
    incoming = incoming.reshape(peers, padded)[:, :row_size]
    take = match.astype(jnp.bfloat16)
    dealt_rows = jnp.einsum(
        "pi,px->ix", take, incoming, preferred_element_type=jnp.float32
    ).astype(jnp.bfloat16)
    rows = slot_count * verified
    lanes = rows * width // 128
    copies = jnp.broadcast_to(dealt_rows.reshape(1, lanes, 128), (shards, lanes, 128))
    features = lax.all_to_all(copies, "tp", 0, 0, tiled=True)
    features = features.reshape(shards, rows, width)
    widened = features.astype(jnp.float32)
    variance = jnp.mean(widened * widened, axis=(0, 2), keepdims=True)
    gain = norm_gain.reshape(shards, 1, width).astype(jnp.float32)
    normed = (widened * lax.rsqrt(variance + 1e-05) * gain).astype(jnp.bfloat16)
    heads_here = query_weight.shape[1] // HEAD_SIZE
    groups_here = key_value_matrix.shape[1]
    positions = cache_length[:, None] + jnp.arange(verified, dtype=jnp.int32)[None, :]
    query_rows = jnp.einsum(
        "knf,kfe->ne",
        normed,
        query_weight.reshape(shards, width, -1),
        preferred_element_type=jnp.float32,
    )
    query_rows = query_rows.reshape(
        slot_count, verified, groups_here, heads_here // groups_here, HEAD_SIZE
    )
    query_rows = rotate(query_rows, positions[:, :, None, None]).astype(jnp.bfloat16)
    projected = jnp.einsum(
        "knf,kfge->nge",
        normed,
        key_value_matrix.reshape(shards, width, groups_here, -1),
        preferred_element_type=jnp.float32,
    ).reshape(slot_count, verified, groups_here, -1)
    fresh = jnp.concatenate(
        [rotate(projected[..., :HEAD_SIZE], positions[:, :, None]), projected[..., HEAD_SIZE:]],
        axis=-1,
    ).astype(jnp.bfloat16)
    keep = (jnp.arange(verified, dtype=jnp.int32)[None, :] < accepted[:, None])[:, :, None, None]
    new_entries = jnp.where(keep, fresh, jnp.zeros_like(fresh))
    mixed = attend(query_rows, key_value_cache, fresh, cache_length)
    partial_sum = jnp.einsum(
        "ne,ekf->knf",
        mixed.reshape(rows, -1),
        output_weight.reshape(-1, shards, width),
        preferred_element_type=jnp.float32,
    )
    pieces = partial_sum.astype(jnp.bfloat16).reshape(shards, lanes, 128)
    pieces = lax.all_to_all(pieces, "tp", 0, 0, tiled=True)
    out_dealt = jnp.sum(pieces.astype(jnp.float32), axis=0)
    out_dealt = out_dealt.reshape(slot_count, verified, width).astype(jnp.bfloat16)
    back_out = jnp.einsum(
        "pi,ix->px", take, out_dealt.reshape(slot_count, row_size), preferred_element_type=jnp.float32
    ).astype(jnp.bfloat16)
    back_out = jnp.pad(back_out, ((0, 0), (0, padded - row_size))).reshape(peers, padded // 128, 128)
    returned = lax.all_to_all(back_out, "req", 0, 0, tiled=True)
    returned = returned.reshape(peers, padded)[:, :row_size]
    block_output = jnp.einsum(
        "dj,dx->jx", pick, returned, preferred_element_type=jnp.float32
    ).astype(jnp.bfloat16).reshape(slot_count, verified, width)
    return (block_output, new_entries)


def solution(mesh):
    placed = (
        P("req", None, "tp"),
        P(),
        P(None, "tp"),
        P(None, "tp", None),
        P("tp", None),
        P("req", None, "tp", None),
        P("req"),
        P("req"),
        P("req"),
    )
    return jax.shard_map(
        functools.partial(body, peers=mesh.shape["req"], shards=mesh.shape["tp"]),
        mesh=mesh,
        in_specs=placed,
        out_specs=(P("req", None, "tp"), P("req", None, "tp", None)),
        check_vma=False,
    )
```

```python
import functools
import math

import jax
import jax.numpy as jnp
from jax import lax
from jax.sharding import PartitionSpec as P

HEAD_SIZE = 80


masked_score = -1e30


def turning(positions):
    half_dim = HEAD_SIZE // 2
    frequency = 10000.0 ** (-2.0 * jnp.arange(half_dim, dtype=jnp.float32) / HEAD_SIZE)
    angles = positions.astype(jnp.float32)[..., None] * frequency
    return jnp.cos(angles), jnp.sin(angles)


def rotate(values, cosine_part, sine_part):
    half_dim = HEAD_SIZE // 2
    first_half = values[..., :half_dim]
    second_half = values[..., half_dim:]
    return jnp.concatenate(
        [
            first_half * cosine_part - second_half * sine_part,
            second_half * cosine_part + first_half * sine_part,
        ],
        axis=-1,
    )


def attend(query_rows, key_value_cache, fresh, visible, causal):
    scale = 1.0 / math.sqrt(HEAD_SIZE)
    slot_count = query_rows.shape[0]
    verified = query_rows.shape[1]
    cache_keys = key_value_cache[..., :HEAD_SIZE]
    cache_values = key_value_cache[..., HEAD_SIZE:]
    fresh_keys = fresh[..., :HEAD_SIZE]
    fresh_values = fresh[..., HEAD_SIZE:]
    cache_scores = (
        jnp.einsum("rtghd,rcgd->rghtc", query_rows, cache_keys, preferred_element_type=jnp.float32)
        * scale
    )
    cache_scores = jnp.where(visible[:, None, None, None, :], cache_scores, masked_score)
    fresh_scores = (
        jnp.einsum("rtghd,rugd->rghtu", query_rows, fresh_keys, preferred_element_type=jnp.float32)
        * scale
    )
    fresh_scores = jnp.where(causal[None, None, None, :, :], fresh_scores, masked_score)
    largest = jnp.maximum(jnp.max(cache_scores, axis=-1), jnp.max(fresh_scores, axis=-1))[..., None]
    cache_expos = jnp.exp(cache_scores - largest)
    fresh_expos = jnp.exp(fresh_scores - largest)
    totals = jnp.sum(cache_expos, axis=-1, keepdims=True) + jnp.sum(
        fresh_expos, axis=-1, keepdims=True
    )
    cache_weights = (cache_expos / totals).astype(jnp.bfloat16)
    fresh_weights = (fresh_expos / totals).astype(jnp.bfloat16)
    mixed = jnp.einsum(
        "rghtc,rcgd->rtghd", cache_weights, cache_values, preferred_element_type=jnp.float32
    )
    mixed = mixed + jnp.einsum(
        "rghtu,rugd->rtghd", fresh_weights, fresh_values, preferred_element_type=jnp.float32
    )
    return mixed.astype(jnp.bfloat16).reshape(slot_count, verified, -1)


def body(
    hidden,
    norm_gain,
    query_weight,
    key_value_matrix,
    output_weight,
    key_value_cache,
    deal_order,
    cache_length,
    accepted,
    *,
    peers,
    shards,
):
    slot_count = deal_order.shape[0]
    verified = hidden.shape[1]
    width = hidden.shape[2]
    source = deal_order // slot_count
    local = deal_order % slot_count
    match = source[None, :] == jnp.arange(peers, dtype=jnp.int32)[:, None]
    wish = jnp.sum(jnp.where(match, local[None, :] + 1, 0), axis=1) - 1
    wanted = lax.all_to_all(wish, "req", 0, 0, tiled=True)
    positions = cache_length[:, None] + jnp.arange(verified, dtype=jnp.int32)[None, :]
    cosine_part, sine_part = turning(positions)
    visible = jnp.arange(key_value_cache.shape[1], dtype=jnp.int32)[None, :] < cache_length[:, None]
    causal = (
        jnp.arange(verified, dtype=jnp.int32)[:, None]
        >= jnp.arange(verified, dtype=jnp.int32)[None, :]
    )
    keep = (jnp.arange(verified, dtype=jnp.int32)[None, :] < accepted[:, None])[:, :, None, None]
    query_t = jnp.transpose(query_weight.reshape(shards, width, -1), (2, 0, 1))
    pair_t = jnp.transpose(key_value_matrix.reshape(shards, width, -1), (2, 0, 1))
    out_w = output_weight.reshape(-1, shards, width)
    gain = norm_gain.reshape(shards, 1, width).astype(jnp.float32)
    held = (wanted, cosine_part, sine_part, visible, causal, keep, query_t, pair_t, out_w, gain, key_value_cache)
    (wanted, cosine_part, sine_part, visible, causal, keep, query_t, pair_t, out_w, gain, key_value_cache) = (
        lax.optimization_barrier(held)
    )
    pick = (wanted[:, None] == jnp.arange(slot_count, dtype=jnp.int32)[None, :]).astype(jnp.bfloat16)
    row_size = verified * width
    tile = 16 * 128
    padded = -(-row_size // tile) * tile
    outgoing = jnp.einsum(
        "dj,jx->dx", pick, hidden.reshape(slot_count, row_size), preferred_element_type=jnp.float32
    ).astype(jnp.bfloat16)
    outgoing = jnp.pad(outgoing, ((0, 0), (0, padded - row_size))).reshape(peers, padded // 128, 128)
    incoming = lax.all_to_all(outgoing, "req", 0, 0, tiled=True)
    incoming = incoming.reshape(peers, padded)[:, :row_size]
    take = match.astype(jnp.bfloat16)
    dealt_rows = jnp.einsum(
        "pi,px->ix", take, incoming, preferred_element_type=jnp.float32
    ).astype(jnp.bfloat16)
    rows = slot_count * verified
    lanes = rows * width // 128
    copies = jnp.broadcast_to(dealt_rows.reshape(1, lanes, 128), (shards, lanes, 128))
    features = lax.all_to_all(copies, "tp", 0, 0, tiled=True)
    features = features.reshape(shards, rows, width)
    widened = features.astype(jnp.float32)
    variance = jnp.mean(widened * widened, axis=(0, 2), keepdims=True)
    normed = (widened * lax.rsqrt(variance + 1e-05) * gain).astype(jnp.bfloat16)
    heads_here = query_weight.shape[1] // HEAD_SIZE
    groups_here = key_value_matrix.shape[1]
    query_rows = jnp.einsum(
        "knf,ekf->ne",
        normed,
        query_t,
        preferred_element_type=jnp.float32,
    )
    query_rows = query_rows.reshape(
        slot_count, verified, groups_here, heads_here // groups_here, HEAD_SIZE
    )
    query_rows = rotate(query_rows, cosine_part[:, :, None, None], sine_part[:, :, None, None]).astype(jnp.bfloat16)
    projected = jnp.einsum(
        "knf,ekf->ne",
        normed,
        pair_t,
        preferred_element_type=jnp.float32,
    ).reshape(slot_count, verified, groups_here, -1)
    fresh = jnp.concatenate(
        [rotate(projected[..., :HEAD_SIZE], cosine_part[:, :, None], sine_part[:, :, None]), projected[..., HEAD_SIZE:]],
        axis=-1,
    ).astype(jnp.bfloat16)
    new_entries = jnp.where(keep, fresh, jnp.zeros_like(fresh))
    mixed = attend(query_rows, key_value_cache, fresh, visible, causal)
    partial_sum = jnp.einsum(
        "ne,ekf->knf",
        mixed.reshape(rows, -1),
        out_w,
        preferred_element_type=jnp.float32,
    )
    pieces = partial_sum.astype(jnp.bfloat16).reshape(shards, lanes, 128)
    pieces, new_entries = lax.optimization_barrier((pieces, new_entries))
    pieces = lax.all_to_all(pieces, "tp", 0, 0, tiled=True)
    out_dealt = jnp.sum(pieces.astype(jnp.float32), axis=0)
    out_dealt = out_dealt.reshape(slot_count, verified, width).astype(jnp.bfloat16)
    back_out = jnp.einsum(
        "pi,ix->px", take, out_dealt.reshape(slot_count, row_size), preferred_element_type=jnp.float32
    ).astype(jnp.bfloat16)
    back_out = jnp.pad(back_out, ((0, 0), (0, padded - row_size))).reshape(peers, padded // 128, 128)
    returned = lax.all_to_all(back_out, "req", 0, 0, tiled=True)
    returned = returned.reshape(peers, padded)[:, :row_size]
    block_output = jnp.einsum(
        "dj,dx->jx", pick, returned, preferred_element_type=jnp.float32
    ).astype(jnp.bfloat16).reshape(slot_count, verified, width)
    return (block_output, new_entries)


def solution(mesh):
    placed = (
        P("req", None, "tp"),
        P(),
        P(None, "tp"),
        P(None, "tp", None),
        P("tp", None),
        P("req", None, "tp", None),
        P("req"),
        P("req"),
        P("req"),
    )
    return jax.shard_map(
        functools.partial(body, peers=mesh.shape["req"], shards=mesh.shape["tp"]),
        mesh=mesh,
        in_specs=placed,
        out_specs=(P("req", None, "tp"), P("req", None, "tp", None)),
        check_vma=False,
    )
```

```python
import functools
import math

import jax
import jax.numpy as jnp
from jax import lax
from jax.sharding import PartitionSpec as P

HEAD_SIZE = 80


masked_score = -1e30


def turning(positions):
    half_dim = HEAD_SIZE // 2
    frequency = 10000.0 ** (-2.0 * jnp.arange(half_dim, dtype=jnp.float32) / HEAD_SIZE)
    angles = positions.astype(jnp.float32)[..., None] * frequency
    return jnp.cos(angles), jnp.sin(angles)


def rotate(values, cosine_part, sine_part):
    half_dim = HEAD_SIZE // 2
    first_half = values[..., :half_dim]
    second_half = values[..., half_dim:]
    return jnp.concatenate(
        [
            first_half * cosine_part - second_half * sine_part,
            second_half * cosine_part + first_half * sine_part,
        ],
        axis=-1,
    )


def attend(query_rows, key_value_cache, fresh, visible, causal):
    scale = 1.0 / math.sqrt(HEAD_SIZE)
    slot_count = query_rows.shape[0]
    verified = query_rows.shape[1]
    cache_keys = key_value_cache[..., :HEAD_SIZE]
    cache_values = key_value_cache[..., HEAD_SIZE:]
    fresh_keys = fresh[..., :HEAD_SIZE]
    fresh_values = fresh[..., HEAD_SIZE:]
    cache_scores = (
        jnp.einsum("rtghd,rcgd->rghtc", query_rows, cache_keys, preferred_element_type=jnp.float32)
        * scale
    )
    cache_scores = jnp.where(visible[:, None, None, None, :], cache_scores, masked_score)
    fresh_scores = (
        jnp.einsum("rtghd,rugd->rghtu", query_rows, fresh_keys, preferred_element_type=jnp.float32)
        * scale
    )
    fresh_scores = jnp.where(causal[None, None, None, :, :], fresh_scores, masked_score)
    largest = jnp.maximum(jnp.max(cache_scores, axis=-1), jnp.max(fresh_scores, axis=-1))[..., None]
    cache_expos = jnp.exp(cache_scores - largest)
    fresh_expos = jnp.exp(fresh_scores - largest)
    totals = jnp.sum(cache_expos, axis=-1, keepdims=True) + jnp.sum(
        fresh_expos, axis=-1, keepdims=True
    )
    cache_weights = (cache_expos / totals).astype(jnp.bfloat16)
    fresh_weights = (fresh_expos / totals).astype(jnp.bfloat16)
    mixed = jnp.einsum(
        "rghtc,rcgd->rtghd", cache_weights, cache_values, preferred_element_type=jnp.float32
    )
    mixed = mixed + jnp.einsum(
        "rghtu,rugd->rtghd", fresh_weights, fresh_values, preferred_element_type=jnp.float32
    )
    return mixed.astype(jnp.bfloat16).reshape(slot_count, verified, -1)


def body(
    hidden,
    norm_gain,
    query_weight,
    key_value_matrix,
    output_weight,
    key_value_cache,
    deal_order,
    cache_length,
    accepted,
    *,
    peers,
    shards,
):
    slot_count = deal_order.shape[0]
    verified = hidden.shape[1]
    width = hidden.shape[2]
    source = deal_order // slot_count
    local = deal_order % slot_count
    match = source[None, :] == jnp.arange(peers, dtype=jnp.int32)[:, None]
    wish = jnp.sum(jnp.where(match, local[None, :] + 1, 0), axis=1) - 1
    wanted = lax.all_to_all(wish, "req", 0, 0, tiled=True)
    positions = cache_length[:, None] + jnp.arange(verified, dtype=jnp.int32)[None, :]
    cosine_part, sine_part = turning(positions)
    visible = jnp.arange(key_value_cache.shape[1], dtype=jnp.int32)[None, :] < cache_length[:, None]
    causal = (
        jnp.arange(verified, dtype=jnp.int32)[:, None]
        >= jnp.arange(verified, dtype=jnp.int32)[None, :]
    )
    keep = (jnp.arange(verified, dtype=jnp.int32)[None, :] < accepted[:, None])[:, :, None, None]
    pair_w = key_value_matrix.reshape(key_value_matrix.shape[0], -1)
    gain = norm_gain.astype(jnp.float32)
    held = (wanted, cosine_part, sine_part, visible, causal, keep, gain, key_value_cache)
    (wanted, cosine_part, sine_part, visible, causal, keep, gain, key_value_cache) = (
        lax.optimization_barrier(held)
    )
    pick = (wanted[:, None] == jnp.arange(slot_count, dtype=jnp.int32)[None, :]).astype(jnp.bfloat16)
    row_size = verified * width
    tile = 16 * 128
    padded = -(-row_size // tile) * tile
    outgoing = jnp.einsum(
        "dj,jx->dx", pick, hidden.reshape(slot_count, row_size), preferred_element_type=jnp.float32
    ).astype(jnp.bfloat16)
    outgoing = jnp.pad(outgoing, ((0, 0), (0, padded - row_size))).reshape(peers, padded // 128, 128)
    incoming = lax.all_to_all(outgoing, "req", 0, 0, tiled=True)
    incoming = incoming.reshape(peers, padded)[:, :row_size]
    take = match.astype(jnp.bfloat16)
    dealt_rows = jnp.einsum(
        "pi,px->ix", take, incoming, preferred_element_type=jnp.float32
    ).astype(jnp.bfloat16)
    rows = slot_count * verified
    lanes = rows * width // 128
    copies = jnp.broadcast_to(dealt_rows.reshape(1, lanes, 128), (shards, lanes, 128))
    features = lax.all_to_all(copies, "tp", 0, 0, tiled=True)
    features = features.reshape(shards, rows, width)
    widened = jnp.transpose(features.astype(jnp.float32), (1, 0, 2)).reshape(rows, shards * width)
    variance = jnp.mean(widened * widened, axis=1, keepdims=True)
    normed = (widened * lax.rsqrt(variance + 1e-05) * gain).astype(jnp.bfloat16)
    heads_here = query_weight.shape[1] // HEAD_SIZE
    groups_here = key_value_matrix.shape[1]
    query_rows = jnp.einsum(
        "nd,de->ne", normed, query_weight, preferred_element_type=jnp.float32
    )
    query_rows = query_rows.reshape(
        slot_count, verified, groups_here, heads_here // groups_here, HEAD_SIZE
    )
    query_rows = rotate(query_rows, cosine_part[:, :, None, None], sine_part[:, :, None, None]).astype(jnp.bfloat16)
    projected = jnp.einsum(
        "nd,de->ne",
        normed,
        pair_w,
        preferred_element_type=jnp.float32,
    ).reshape(slot_count, verified, groups_here, -1)
    fresh = jnp.concatenate(
        [rotate(projected[..., :HEAD_SIZE], cosine_part[:, :, None], sine_part[:, :, None]), projected[..., HEAD_SIZE:]],
        axis=-1,
    ).astype(jnp.bfloat16)
    new_entries = jnp.where(keep, fresh, jnp.zeros_like(fresh))
    mixed = attend(query_rows, key_value_cache, fresh, visible, causal)
    partial_sum = jnp.einsum(
        "ne,ed->nd", mixed.reshape(rows, -1), output_weight, preferred_element_type=jnp.float32
    )
    partial_sum = jnp.transpose(partial_sum.reshape(rows, shards, width), (1, 0, 2))
    pieces = partial_sum.astype(jnp.bfloat16).reshape(shards, lanes, 128)
    pieces, new_entries = lax.optimization_barrier((pieces, new_entries))
    pieces = lax.all_to_all(pieces, "tp", 0, 0, tiled=True)
    out_dealt = jnp.sum(pieces.astype(jnp.float32), axis=0)
    out_dealt = out_dealt.reshape(slot_count, verified, width).astype(jnp.bfloat16)
    back_out = jnp.einsum(
        "pi,ix->px", take, out_dealt.reshape(slot_count, row_size), preferred_element_type=jnp.float32
    ).astype(jnp.bfloat16)
    back_out = jnp.pad(back_out, ((0, 0), (0, padded - row_size))).reshape(peers, padded // 128, 128)
    returned = lax.all_to_all(back_out, "req", 0, 0, tiled=True)
    returned = returned.reshape(peers, padded)[:, :row_size]
    block_output = jnp.einsum(
        "dj,dx->jx", pick, returned, preferred_element_type=jnp.float32
    ).astype(jnp.bfloat16).reshape(slot_count, verified, width)
    return (block_output, new_entries)


def solution(mesh):
    placed = (
        P("req", None, "tp"),
        P(),
        P(None, "tp"),
        P(None, "tp", None),
        P("tp", None),
        P("req", None, "tp", None),
        P("req"),
        P("req"),
        P("req"),
    )
    return jax.shard_map(
        functools.partial(body, peers=mesh.shape["req"], shards=mesh.shape["tp"]),
        mesh=mesh,
        in_specs=placed,
        out_specs=(P("req", None, "tp"), P("req", None, "tp", None)),
        check_vma=False,
    )
```

```python
import functools
import math

import jax
import jax.numpy as jnp
from jax import lax
from jax.sharding import PartitionSpec as P

HEAD_SIZE = 80


masked_score = -1e30


def turning(positions):
    half_dim = HEAD_SIZE // 2
    frequency = 10000.0 ** (-2.0 * jnp.arange(half_dim, dtype=jnp.float32) / HEAD_SIZE)
    angles = positions.astype(jnp.float32)[..., None] * frequency
    return jnp.cos(angles), jnp.sin(angles)


def rotate(values, cosine_part, sine_part):
    half_dim = HEAD_SIZE // 2
    first_half = values[..., :half_dim]
    second_half = values[..., half_dim:]
    return jnp.concatenate(
        [
            first_half * cosine_part - second_half * sine_part,
            second_half * cosine_part + first_half * sine_part,
        ],
        axis=-1,
    )


def attend(query_rows, key_value_cache, fresh, visible, causal):
    scale = 1.0 / math.sqrt(HEAD_SIZE)
    slot_count = query_rows.shape[0]
    verified = query_rows.shape[1]
    cache_keys = key_value_cache[..., :HEAD_SIZE]
    cache_values = key_value_cache[..., HEAD_SIZE:]
    fresh_keys = fresh[..., :HEAD_SIZE]
    fresh_values = fresh[..., HEAD_SIZE:]
    cache_scores = (
        jnp.einsum("rtghd,rcgd->rghtc", query_rows, cache_keys, preferred_element_type=jnp.float32)
        * scale
    )
    cache_scores = jnp.where(visible[:, None, None, None, :], cache_scores, masked_score)
    fresh_scores = (
        jnp.einsum("rtghd,rugd->rghtu", query_rows, fresh_keys, preferred_element_type=jnp.float32)
        * scale
    )
    fresh_scores = jnp.where(causal[None, None, None, :, :], fresh_scores, masked_score)
    largest = jnp.maximum(jnp.max(cache_scores, axis=-1), jnp.max(fresh_scores, axis=-1))[..., None]
    cache_expos = jnp.exp(cache_scores - largest)
    fresh_expos = jnp.exp(fresh_scores - largest)
    totals = jnp.sum(cache_expos, axis=-1, keepdims=True) + jnp.sum(
        fresh_expos, axis=-1, keepdims=True
    )
    cache_weights = (cache_expos / totals).astype(jnp.bfloat16)
    fresh_weights = (fresh_expos / totals).astype(jnp.bfloat16)
    mixed = jnp.einsum(
        "rghtc,rcgd->rtghd", cache_weights, cache_values, preferred_element_type=jnp.float32
    )
    mixed = mixed + jnp.einsum(
        "rghtu,rugd->rtghd", fresh_weights, fresh_values, preferred_element_type=jnp.float32
    )
    return mixed.astype(jnp.bfloat16).reshape(slot_count, verified, -1)


def body(
    hidden,
    norm_gain,
    query_weight,
    key_value_matrix,
    output_weight,
    key_value_cache,
    deal_order,
    cache_length,
    accepted,
    *,
    peers,
    shards,
):
    slot_count = deal_order.shape[0]
    verified = hidden.shape[1]
    width = hidden.shape[2]
    source = deal_order // slot_count
    local = deal_order % slot_count
    match = source[None, :] == jnp.arange(peers, dtype=jnp.int32)[:, None]
    wish = jnp.sum(jnp.where(match, local[None, :] + 1, 0), axis=1) - 1
    wanted = lax.all_to_all(wish, "req", 0, 0, tiled=True)
    positions = cache_length[:, None] + jnp.arange(verified, dtype=jnp.int32)[None, :]
    cosine_part, sine_part = turning(positions)
    visible = jnp.arange(key_value_cache.shape[1], dtype=jnp.int32)[None, :] < cache_length[:, None]
    causal = (
        jnp.arange(verified, dtype=jnp.int32)[:, None]
        >= jnp.arange(verified, dtype=jnp.int32)[None, :]
    )
    keep = (jnp.arange(verified, dtype=jnp.int32)[None, :] < accepted[:, None])[:, :, None, None]
    gain = norm_gain.reshape(shards, 1, width).astype(jnp.float32)
    held = (wanted, cosine_part, sine_part, visible, causal, keep, gain)
    (wanted, cosine_part, sine_part, visible, causal, keep, gain) = lax.optimization_barrier(held)
    pick = (wanted[:, None] == jnp.arange(slot_count, dtype=jnp.int32)[None, :]).astype(jnp.bfloat16)
    row_size = verified * width
    tile = 16 * 128
    padded = -(-row_size // tile) * tile
    outgoing = jnp.einsum(
        "dj,jx->dx", pick, hidden.reshape(slot_count, row_size), preferred_element_type=jnp.float32
    ).astype(jnp.bfloat16)
    outgoing = jnp.pad(outgoing, ((0, 0), (0, padded - row_size))).reshape(peers, padded // 128, 128)
    incoming = lax.all_to_all(outgoing, "req", 0, 0, tiled=True)
    incoming = incoming.reshape(peers, padded)[:, :row_size]
    take = match.astype(jnp.bfloat16)
    dealt_rows = jnp.einsum(
        "pi,px->ix", take, incoming, preferred_element_type=jnp.float32
    ).astype(jnp.bfloat16)
    rows = slot_count * verified
    lanes = rows * width // 128
    features = lax.all_gather(dealt_rows.reshape(lanes, 128), "tp", axis=0, tiled=False)
    features = features.reshape(shards, rows, width)
    widened = features.astype(jnp.float32)
    variance = jnp.mean(widened * widened, axis=(0, 2), keepdims=True)
    normed = (widened * lax.rsqrt(variance + 1e-05) * gain).astype(jnp.bfloat16)
    heads_here = query_weight.shape[1] // HEAD_SIZE
    groups_here = key_value_matrix.shape[1]
    query_rows = jnp.einsum(
        "knf,kfe->ne",
        normed,
        query_weight.reshape(shards, width, -1),
        preferred_element_type=jnp.float32,
    )
    query_rows = query_rows.reshape(
        slot_count, verified, groups_here, heads_here // groups_here, HEAD_SIZE
    )
    query_rows = rotate(query_rows, cosine_part[:, :, None, None], sine_part[:, :, None, None]).astype(jnp.bfloat16)
    projected = jnp.einsum(
        "knf,kfge->nge",
        normed,
        key_value_matrix.reshape(shards, width, groups_here, -1),
        preferred_element_type=jnp.float32,
    ).reshape(slot_count, verified, groups_here, -1)
    fresh = jnp.concatenate(
        [rotate(projected[..., :HEAD_SIZE], cosine_part[:, :, None], sine_part[:, :, None]), projected[..., HEAD_SIZE:]],
        axis=-1,
    ).astype(jnp.bfloat16)
    new_entries = jnp.where(keep, fresh, jnp.zeros_like(fresh))
    mixed = attend(query_rows, key_value_cache, fresh, visible, causal)
    partial_sum = jnp.einsum(
        "ne,ekf->knf",
        mixed.reshape(rows, -1),
        output_weight.reshape(-1, shards, width),
        preferred_element_type=jnp.float32,
    )
    pieces = partial_sum.astype(jnp.bfloat16).reshape(shards, lanes, 128)
    pieces = lax.all_to_all(pieces, "tp", 0, 0, tiled=True)
    out_dealt = jnp.sum(pieces.astype(jnp.float32), axis=0)
    out_dealt = out_dealt.reshape(slot_count, verified, width).astype(jnp.bfloat16)
    back_out = jnp.einsum(
        "pi,ix->px", take, out_dealt.reshape(slot_count, row_size), preferred_element_type=jnp.float32
    ).astype(jnp.bfloat16)
    back_out = jnp.pad(back_out, ((0, 0), (0, padded - row_size))).reshape(peers, padded // 128, 128)
    returned = lax.all_to_all(back_out, "req", 0, 0, tiled=True)
    returned = returned.reshape(peers, padded)[:, :row_size]
    block_output = jnp.einsum(
        "dj,dx->jx", pick, returned, preferred_element_type=jnp.float32
    ).astype(jnp.bfloat16).reshape(slot_count, verified, width)
    return (block_output, new_entries)


def solution(mesh):
    placed = (
        P("req", None, "tp"),
        P(),
        P(None, "tp"),
        P(None, "tp", None),
        P("tp", None),
        P("req", None, "tp", None),
        P("req"),
        P("req"),
        P("req"),
    )
    return jax.shard_map(
        functools.partial(body, peers=mesh.shape["req"], shards=mesh.shape["tp"]),
        mesh=mesh,
        in_specs=placed,
        out_specs=(P("req", None, "tp"), P("req", None, "tp", None)),
        check_vma=False,
    )
```

```python
import functools
import math

import jax
import jax.numpy as jnp
from jax import lax
from jax.sharding import Mesh, PartitionSpec as P

HEAD_SIZE = 80


masked_score = -1e30


def turning(positions):
    half_dim = HEAD_SIZE // 2
    frequency = 10000.0 ** (-2.0 * jnp.arange(half_dim, dtype=jnp.float32) / HEAD_SIZE)
    angles = positions.astype(jnp.float32)[..., None] * frequency
    return jnp.cos(angles), jnp.sin(angles)


def rotate(values, cosine_part, sine_part):
    half_dim = HEAD_SIZE // 2
    first_half = values[..., :half_dim]
    second_half = values[..., half_dim:]
    return jnp.concatenate(
        [
            first_half * cosine_part - second_half * sine_part,
            second_half * cosine_part + first_half * sine_part,
        ],
        axis=-1,
    )


def attend(query_rows, key_value_cache, fresh, visible, causal):
    scale = 1.0 / math.sqrt(HEAD_SIZE)
    slot_count = query_rows.shape[0]
    verified = query_rows.shape[1]
    cache_keys = key_value_cache[..., :HEAD_SIZE]
    cache_values = key_value_cache[..., HEAD_SIZE:]
    fresh_keys = fresh[..., :HEAD_SIZE]
    fresh_values = fresh[..., HEAD_SIZE:]
    cache_scores = (
        jnp.einsum("rtghd,rcgd->rghtc", query_rows, cache_keys, preferred_element_type=jnp.float32)
        * scale
    )
    cache_scores = jnp.where(visible[:, None, None, None, :], cache_scores, masked_score)
    fresh_scores = (
        jnp.einsum("rtghd,rugd->rghtu", query_rows, fresh_keys, preferred_element_type=jnp.float32)
        * scale
    )
    fresh_scores = jnp.where(causal[None, None, None, :, :], fresh_scores, masked_score)
    largest = jnp.maximum(jnp.max(cache_scores, axis=-1), jnp.max(fresh_scores, axis=-1))[..., None]
    cache_expos = jnp.exp(cache_scores - largest)
    fresh_expos = jnp.exp(fresh_scores - largest)
    totals = jnp.sum(cache_expos, axis=-1, keepdims=True) + jnp.sum(
        fresh_expos, axis=-1, keepdims=True
    )
    cache_weights = (cache_expos / totals).astype(jnp.bfloat16)
    fresh_weights = (fresh_expos / totals).astype(jnp.bfloat16)
    mixed = jnp.einsum(
        "rghtc,rcgd->rtghd", cache_weights, cache_values, preferred_element_type=jnp.float32
    )
    mixed = mixed + jnp.einsum(
        "rghtu,rugd->rtghd", fresh_weights, fresh_values, preferred_element_type=jnp.float32
    )
    return mixed.astype(jnp.bfloat16).reshape(slot_count, verified, -1)


def body(
    hidden,
    norm_gain,
    query_weight,
    key_value_matrix,
    output_weight,
    key_value_cache,
    deal_order,
    cache_length,
    accepted,
    *,
    peers,
    shards,
):
    slot_count = deal_order.shape[0]
    verified = hidden.shape[1]
    width = hidden.shape[2]
    source = deal_order // slot_count
    local = deal_order % slot_count
    match = source[None, :] == jnp.arange(peers, dtype=jnp.int32)[:, None]
    wish = jnp.sum(jnp.where(match, local[None, :] + 1, 0), axis=1) - 1
    wanted = lax.all_to_all(wish, "req", 0, 0, tiled=True)
    positions = cache_length[:, None] + jnp.arange(verified, dtype=jnp.int32)[None, :]
    cosine_part, sine_part = turning(positions)
    visible = jnp.arange(key_value_cache.shape[1], dtype=jnp.int32)[None, :] < cache_length[:, None]
    causal = (
        jnp.arange(verified, dtype=jnp.int32)[:, None]
        >= jnp.arange(verified, dtype=jnp.int32)[None, :]
    )
    keep = (jnp.arange(verified, dtype=jnp.int32)[None, :] < accepted[:, None])[:, :, None, None]
    gain = norm_gain.reshape(shards, 1, width).astype(jnp.float32)
    held = (wanted, cosine_part, sine_part, visible, causal, keep, gain)
    (wanted, cosine_part, sine_part, visible, causal, keep, gain) = lax.optimization_barrier(held)
    pick = (wanted[:, None] == jnp.arange(slot_count, dtype=jnp.int32)[None, :]).astype(jnp.bfloat16)
    row_size = verified * width
    tile = 16 * 128
    padded = -(-row_size // tile) * tile
    partner = lax.ppermute(hidden, "tp_lo", [(0, 1), (1, 0)])
    low = lax.axis_index("tp_lo")
    pair = jnp.where(low == 0, jnp.stack([hidden, partner]), jnp.stack([partner, hidden]))
    outgoing = jnp.einsum(
        "dj,qjx->dqx", pick, pair.reshape(2, slot_count, row_size), preferred_element_type=jnp.float32
    ).astype(jnp.bfloat16)
    outgoing = jnp.pad(outgoing, ((0, 0), (0, 0), (0, padded - row_size))).reshape(peers, 2 * padded // 128, 128)
    incoming = lax.all_to_all(outgoing, "req", 0, 0, tiled=True)
    incoming = incoming.reshape(peers, 2, padded)[:, :, :row_size]
    take = match.astype(jnp.bfloat16)
    dealt_rows = jnp.einsum(
        "pi,pqx->qix", take, incoming, preferred_element_type=jnp.float32
    ).astype(jnp.bfloat16)
    rows = slot_count * verified
    lanes = rows * width // 128
    features = lax.all_gather(dealt_rows.reshape(2, lanes, 128), "tp_hi", axis=0, tiled=False)
    features = features.reshape(shards, rows, width)
    widened = features.astype(jnp.float32)
    variance = jnp.mean(widened * widened, axis=(0, 2), keepdims=True)
    normed = (widened * lax.rsqrt(variance + 1e-05) * gain).astype(jnp.bfloat16)
    heads_here = query_weight.shape[1] // HEAD_SIZE
    groups_here = key_value_matrix.shape[1]
    query_rows = jnp.einsum(
        "knf,kfe->ne",
        normed,
        query_weight.reshape(shards, width, -1),
        preferred_element_type=jnp.float32,
    )
    query_rows = query_rows.reshape(
        slot_count, verified, groups_here, heads_here // groups_here, HEAD_SIZE
    )
    query_rows = rotate(query_rows, cosine_part[:, :, None, None], sine_part[:, :, None, None]).astype(jnp.bfloat16)
    projected = jnp.einsum(
        "knf,kfge->nge",
        normed,
        key_value_matrix.reshape(shards, width, groups_here, -1),
        preferred_element_type=jnp.float32,
    ).reshape(slot_count, verified, groups_here, -1)
    fresh = jnp.concatenate(
        [rotate(projected[..., :HEAD_SIZE], cosine_part[:, :, None], sine_part[:, :, None]), projected[..., HEAD_SIZE:]],
        axis=-1,
    ).astype(jnp.bfloat16)
    new_entries = jnp.where(keep, fresh, jnp.zeros_like(fresh))
    mixed = attend(query_rows, key_value_cache, fresh, visible, causal)
    partial_sum = jnp.einsum(
        "ne,ekf->knf",
        mixed.reshape(rows, -1),
        output_weight.reshape(-1, shards, width),
        preferred_element_type=jnp.float32,
    )
    pieces = partial_sum.astype(jnp.bfloat16).reshape(shards, lanes, 128)
    pieces = lax.all_to_all(pieces, ("tp_hi", "tp_lo"), 0, 0, tiled=True)
    out_dealt = jnp.sum(pieces.astype(jnp.float32), axis=0)
    out_dealt = out_dealt.reshape(slot_count, verified, width).astype(jnp.bfloat16)
    back_out = jnp.einsum(
        "pi,ix->px", take, out_dealt.reshape(slot_count, row_size), preferred_element_type=jnp.float32
    ).astype(jnp.bfloat16)
    back_out = jnp.pad(back_out, ((0, 0), (0, padded - row_size))).reshape(peers, padded // 128, 128)
    returned = lax.all_to_all(back_out, "req", 0, 0, tiled=True)
    returned = returned.reshape(peers, padded)[:, :row_size]
    block_output = jnp.einsum(
        "dj,dx->jx", pick, returned, preferred_element_type=jnp.float32
    ).astype(jnp.bfloat16).reshape(slot_count, verified, width)
    return (block_output, new_entries)


def solution(mesh):
    req, tp = mesh.shape["req"], mesh.shape["tp"]
    split = Mesh(mesh.devices.reshape(req, tp // 2, 2), ("req", "tp_hi", "tp_lo"))
    both = ("tp_hi", "tp_lo")
    placed = (
        P("req", None, both),
        P(),
        P(None, both),
        P(None, both, None),
        P(both, None),
        P("req", None, both, None),
        P("req"),
        P("req"),
        P("req"),
    )
    return jax.shard_map(
        functools.partial(body, peers=req, shards=tp),
        mesh=split,
        in_specs=placed,
        out_specs=(P("req", None, both), P("req", None, both, None)),
        check_vma=False,
    )
```

```python
import functools
import math

import jax
import jax.numpy as jnp
from jax import lax
from jax.sharding import PartitionSpec as P

HEAD_SIZE = 80


masked_score = -1e30


def turning(positions):
    half_dim = HEAD_SIZE // 2
    frequency = 10000.0 ** (-2.0 * jnp.arange(half_dim, dtype=jnp.float32) / HEAD_SIZE)
    angles = positions.astype(jnp.float32)[..., None] * frequency
    return jnp.cos(angles), jnp.sin(angles)


def rotate(values, cosine_part, sine_part):
    half_dim = HEAD_SIZE // 2
    first_half = values[..., :half_dim]
    second_half = values[..., half_dim:]
    return jnp.concatenate(
        [
            first_half * cosine_part - second_half * sine_part,
            second_half * cosine_part + first_half * sine_part,
        ],
        axis=-1,
    )


def attend(query_rows, key_value_cache, fresh, visible, causal):
    scale = 1.0 / math.sqrt(HEAD_SIZE)
    slot_count = query_rows.shape[0]
    verified = query_rows.shape[1]
    cache_keys = key_value_cache[..., :HEAD_SIZE]
    cache_values = key_value_cache[..., HEAD_SIZE:]
    fresh_keys = fresh[..., :HEAD_SIZE]
    fresh_values = fresh[..., HEAD_SIZE:]
    cache_scores = (
        jnp.einsum("rtghd,rcgd->rghtc", query_rows, cache_keys, preferred_element_type=jnp.float32)
        * scale
    )
    cache_scores = jnp.where(visible[:, None, None, None, :], cache_scores, masked_score)
    fresh_scores = (
        jnp.einsum("rtghd,rugd->rghtu", query_rows, fresh_keys, preferred_element_type=jnp.float32)
        * scale
    )
    fresh_scores = jnp.where(causal[None, None, None, :, :], fresh_scores, masked_score)
    largest = jnp.maximum(jnp.max(cache_scores, axis=-1), jnp.max(fresh_scores, axis=-1))[..., None]
    cache_expos = jnp.exp(cache_scores - largest)
    fresh_expos = jnp.exp(fresh_scores - largest)
    totals = jnp.sum(cache_expos, axis=-1, keepdims=True) + jnp.sum(
        fresh_expos, axis=-1, keepdims=True
    )
    cache_weights = (cache_expos / totals).astype(jnp.bfloat16)
    fresh_weights = (fresh_expos / totals).astype(jnp.bfloat16)
    mixed = jnp.einsum(
        "rghtc,rcgd->rtghd", cache_weights, cache_values, preferred_element_type=jnp.float32
    )
    mixed = mixed + jnp.einsum(
        "rghtu,rugd->rtghd", fresh_weights, fresh_values, preferred_element_type=jnp.float32
    )
    return mixed.astype(jnp.bfloat16).reshape(slot_count, verified, -1)


def body(
    hidden,
    norm_gain,
    query_weight,
    key_value_matrix,
    output_weight,
    key_value_cache,
    deal_order,
    cache_length,
    accepted,
    *,
    peers,
    shards,
):
    slot_count = deal_order.shape[0]
    verified = hidden.shape[1]
    width = hidden.shape[2]
    source = deal_order // slot_count
    local = deal_order % slot_count
    match = source[None, :] == jnp.arange(peers, dtype=jnp.int32)[:, None]
    wish = jnp.sum(jnp.where(match, local[None, :] + 1, 0), axis=1) - 1
    wanted = lax.all_to_all(wish, "req", 0, 0, tiled=True)
    positions = cache_length[:, None] + jnp.arange(verified, dtype=jnp.int32)[None, :]
    cosine_part, sine_part = turning(positions)
    visible = jnp.arange(key_value_cache.shape[1], dtype=jnp.int32)[None, :] < cache_length[:, None]
    causal = (
        jnp.arange(verified, dtype=jnp.int32)[:, None]
        >= jnp.arange(verified, dtype=jnp.int32)[None, :]
    )
    keep = (jnp.arange(verified, dtype=jnp.int32)[None, :] < accepted[:, None])[:, :, None, None]
    gain = norm_gain.reshape(shards, 1, width).astype(jnp.float32)
    held = (wanted, cosine_part, sine_part, visible, causal, keep, gain)
    (wanted, cosine_part, sine_part, visible, causal, keep, gain) = lax.optimization_barrier(held)
    pick = (wanted[:, None] == jnp.arange(slot_count, dtype=jnp.int32)[None, :]).astype(jnp.bfloat16)
    row_size = verified * width
    tile = 16 * 128
    padded = -(-row_size // tile) * tile
    outgoing = jnp.einsum(
        "dj,jx->dx", pick, hidden.reshape(slot_count, row_size), preferred_element_type=jnp.float32
    ).astype(jnp.bfloat16)
    outgoing = jnp.pad(outgoing, ((0, 0), (0, padded - row_size))).reshape(peers, padded // 128, 128)
    incoming = lax.all_to_all(outgoing, "req", 0, 0, tiled=True)
    incoming = incoming.reshape(peers, padded)[:, :row_size]
    take = match.astype(jnp.bfloat16)
    dealt_rows = jnp.einsum(
        "pi,px->ix", take, incoming, preferred_element_type=jnp.float32
    ).astype(jnp.bfloat16)
    rows = slot_count * verified
    lanes = rows * width // 128
    features = lax.all_gather(dealt_rows.reshape(lanes, 128), "tp", axis=0, tiled=False)
    features = features.reshape(shards, rows, width)
    widened = features.astype(jnp.float32)
    variance = jnp.mean(widened * widened, axis=(0, 2), keepdims=True)
    normed = (widened * lax.rsqrt(variance + 1e-05) * gain).astype(jnp.bfloat16)
    heads_here = query_weight.shape[1] // HEAD_SIZE
    groups_here = key_value_matrix.shape[1]
    query_rows = jnp.einsum(
        "knf,kfe->ne",
        normed,
        query_weight.reshape(shards, width, -1),
        preferred_element_type=jnp.float32,
    )
    query_rows = query_rows.reshape(
        slot_count, verified, groups_here, heads_here // groups_here, HEAD_SIZE
    )
    query_rows = rotate(query_rows, cosine_part[:, :, None, None], sine_part[:, :, None, None]).astype(jnp.bfloat16)
    projected = jnp.einsum(
        "knf,kfge->nge",
        normed,
        key_value_matrix.reshape(shards, width, groups_here, -1),
        preferred_element_type=jnp.float32,
    ).reshape(slot_count, verified, groups_here, -1)
    fresh = jnp.concatenate(
        [rotate(projected[..., :HEAD_SIZE], cosine_part[:, :, None], sine_part[:, :, None]), projected[..., HEAD_SIZE:]],
        axis=-1,
    ).astype(jnp.bfloat16)
    new_entries = jnp.where(keep, fresh, jnp.zeros_like(fresh))
    mixed = attend(query_rows, key_value_cache, fresh, visible, causal)
    partial_sum = jnp.einsum(
        "ne,ekf->knf",
        mixed.reshape(rows, -1),
        output_weight.reshape(-1, shards, width),
        preferred_element_type=jnp.float32,
    )
    pieces = partial_sum.astype(jnp.bfloat16).reshape(shards, lanes, 128)
    pieces, new_entries = lax.optimization_barrier((pieces, new_entries))
    pieces = lax.all_to_all(pieces, "tp", 0, 0, tiled=True)
    out_dealt = jnp.sum(pieces.astype(jnp.float32), axis=0)
    out_dealt = out_dealt.reshape(slot_count, verified, width).astype(jnp.bfloat16)
    back_out = jnp.einsum(
        "pi,ix->px", take, out_dealt.reshape(slot_count, row_size), preferred_element_type=jnp.float32
    ).astype(jnp.bfloat16)
    back_out = jnp.pad(back_out, ((0, 0), (0, padded - row_size))).reshape(peers, padded // 128, 128)
    returned = lax.all_to_all(back_out, "req", 0, 0, tiled=True)
    returned = returned.reshape(peers, padded)[:, :row_size]
    block_output = jnp.einsum(
        "dj,dx->jx", pick, returned, preferred_element_type=jnp.float32
    ).astype(jnp.bfloat16).reshape(slot_count, verified, width)
    return (block_output, new_entries)


def solution(mesh):
    placed = (
        P("req", None, "tp"),
        P(),
        P(None, "tp"),
        P(None, "tp", None),
        P("tp", None),
        P("req", None, "tp", None),
        P("req"),
        P("req"),
        P("req"),
    )
    return jax.shard_map(
        functools.partial(body, peers=mesh.shape["req"], shards=mesh.shape["tp"]),
        mesh=mesh,
        in_specs=placed,
        out_specs=(P("req", None, "tp"), P("req", None, "tp", None)),
        check_vma=False,
    )
```

```python
import functools
import math

import jax
import jax.numpy as jnp
from jax import lax
from jax.sharding import PartitionSpec as P

HEAD_SIZE = 80


masked_score = -1e30


def turning(positions):
    half_dim = HEAD_SIZE // 2
    frequency = 10000.0 ** (-2.0 * jnp.arange(half_dim, dtype=jnp.float32) / HEAD_SIZE)
    angles = positions.astype(jnp.float32)[..., None] * frequency
    return jnp.cos(angles), jnp.sin(angles)


def rotate(values, cosine_part, sine_part):
    half_dim = HEAD_SIZE // 2
    first_half = values[..., :half_dim]
    second_half = values[..., half_dim:]
    return jnp.concatenate(
        [
            first_half * cosine_part - second_half * sine_part,
            second_half * cosine_part + first_half * sine_part,
        ],
        axis=-1,
    )


def attend(query_rows, key_value_cache, fresh, visible, causal):
    scale = 1.0 / math.sqrt(HEAD_SIZE)
    slot_count = query_rows.shape[0]
    verified = query_rows.shape[1]
    entries = jnp.concatenate([key_value_cache, fresh], axis=1)
    keys = entries[..., :HEAD_SIZE]
    values = entries[..., HEAD_SIZE:]
    seen = jnp.concatenate(
        [
            jnp.broadcast_to(visible[:, None, :], (slot_count, verified, visible.shape[1])),
            jnp.broadcast_to(causal[None, :, :], (slot_count, verified, verified)),
        ],
        axis=2,
    )
    scores = (
        jnp.einsum("rtghd,rcgd->rghtc", query_rows, keys, preferred_element_type=jnp.float32)
        * scale
    )
    scores = jnp.where(seen[:, None, None, :, :], scores, masked_score)
    largest = jnp.max(scores, axis=-1, keepdims=True)
    expos = jnp.exp(scores - largest)
    weights = (expos / jnp.sum(expos, axis=-1, keepdims=True)).astype(jnp.bfloat16)
    mixed = jnp.einsum(
        "rghtc,rcgd->rtghd", weights, values, preferred_element_type=jnp.float32
    )
    return mixed.astype(jnp.bfloat16).reshape(slot_count, verified, -1)


def body(
    hidden,
    norm_gain,
    query_weight,
    key_value_matrix,
    output_weight,
    key_value_cache,
    deal_order,
    cache_length,
    accepted,
    *,
    peers,
    shards,
):
    slot_count = deal_order.shape[0]
    verified = hidden.shape[1]
    width = hidden.shape[2]
    source = deal_order // slot_count
    local = deal_order % slot_count
    match = source[None, :] == jnp.arange(peers, dtype=jnp.int32)[:, None]
    wish = jnp.sum(jnp.where(match, local[None, :] + 1, 0), axis=1) - 1
    wanted = lax.all_to_all(wish, "req", 0, 0, tiled=True)
    positions = cache_length[:, None] + jnp.arange(verified, dtype=jnp.int32)[None, :]
    cosine_part, sine_part = turning(positions)
    visible = jnp.arange(key_value_cache.shape[1], dtype=jnp.int32)[None, :] < cache_length[:, None]
    causal = (
        jnp.arange(verified, dtype=jnp.int32)[:, None]
        >= jnp.arange(verified, dtype=jnp.int32)[None, :]
    )
    keep = (jnp.arange(verified, dtype=jnp.int32)[None, :] < accepted[:, None])[:, :, None, None]
    gain = norm_gain.reshape(shards, 1, width).astype(jnp.float32)
    held = (wanted, cosine_part, sine_part, visible, causal, keep, gain)
    (wanted, cosine_part, sine_part, visible, causal, keep, gain) = lax.optimization_barrier(held)
    pick = (wanted[:, None] == jnp.arange(slot_count, dtype=jnp.int32)[None, :]).astype(jnp.bfloat16)
    row_size = verified * width
    tile = 16 * 128
    padded = -(-row_size // tile) * tile
    outgoing = jnp.einsum(
        "dj,jx->dx", pick, hidden.reshape(slot_count, row_size), preferred_element_type=jnp.float32
    ).astype(jnp.bfloat16)
    outgoing = jnp.pad(outgoing, ((0, 0), (0, padded - row_size))).reshape(peers, padded // 128, 128)
    incoming = lax.all_to_all(outgoing, "req", 0, 0, tiled=True)
    incoming = incoming.reshape(peers, padded)[:, :row_size]
    take = match.astype(jnp.bfloat16)
    dealt_rows = jnp.einsum(
        "pi,px->ix", take, incoming, preferred_element_type=jnp.float32
    ).astype(jnp.bfloat16)
    rows = slot_count * verified
    lanes = rows * width // 128
    features = lax.all_gather(dealt_rows.reshape(lanes, 128), "tp", axis=0, tiled=False)
    features = features.reshape(shards, rows, width)
    widened = features.astype(jnp.float32)
    variance = jnp.mean(widened * widened, axis=(0, 2), keepdims=True)
    normed = (widened * lax.rsqrt(variance + 1e-05) * gain).astype(jnp.bfloat16)
    heads_here = query_weight.shape[1] // HEAD_SIZE
    groups_here = key_value_matrix.shape[1]
    query_rows = jnp.einsum(
        "knf,kfe->ne",
        normed,
        query_weight.reshape(shards, width, -1),
        preferred_element_type=jnp.float32,
    )
    query_rows = query_rows.reshape(
        slot_count, verified, groups_here, heads_here // groups_here, HEAD_SIZE
    )
    query_rows = rotate(query_rows, cosine_part[:, :, None, None], sine_part[:, :, None, None]).astype(jnp.bfloat16)
    projected = jnp.einsum(
        "knf,kfge->nge",
        normed,
        key_value_matrix.reshape(shards, width, groups_here, -1),
        preferred_element_type=jnp.float32,
    ).reshape(slot_count, verified, groups_here, -1)
    fresh = jnp.concatenate(
        [rotate(projected[..., :HEAD_SIZE], cosine_part[:, :, None], sine_part[:, :, None]), projected[..., HEAD_SIZE:]],
        axis=-1,
    ).astype(jnp.bfloat16)
    new_entries = jnp.where(keep, fresh, jnp.zeros_like(fresh))
    mixed = attend(query_rows, key_value_cache, fresh, visible, causal)
    partial_sum = jnp.einsum(
        "ne,ekf->knf",
        mixed.reshape(rows, -1),
        output_weight.reshape(-1, shards, width),
        preferred_element_type=jnp.float32,
    )
    pieces = partial_sum.astype(jnp.bfloat16).reshape(shards, lanes, 128)
    pieces, new_entries = lax.optimization_barrier((pieces, new_entries))
    pieces = lax.all_to_all(pieces, "tp", 0, 0, tiled=True)
    out_dealt = jnp.sum(pieces.astype(jnp.float32), axis=0)
    out_dealt = out_dealt.reshape(slot_count, verified, width).astype(jnp.bfloat16)
    back_out = jnp.einsum(
        "pi,ix->px", take, out_dealt.reshape(slot_count, row_size), preferred_element_type=jnp.float32
    ).astype(jnp.bfloat16)
    back_out = jnp.pad(back_out, ((0, 0), (0, padded - row_size))).reshape(peers, padded // 128, 128)
    returned = lax.all_to_all(back_out, "req", 0, 0, tiled=True)
    returned = returned.reshape(peers, padded)[:, :row_size]
    block_output = jnp.einsum(
        "dj,dx->jx", pick, returned, preferred_element_type=jnp.float32
    ).astype(jnp.bfloat16).reshape(slot_count, verified, width)
    return (block_output, new_entries)


def solution(mesh):
    placed = (
        P("req", None, "tp"),
        P(),
        P(None, "tp"),
        P(None, "tp", None),
        P("tp", None),
        P("req", None, "tp", None),
        P("req"),
        P("req"),
        P("req"),
    )
    return jax.shard_map(
        functools.partial(body, peers=mesh.shape["req"], shards=mesh.shape["tp"]),
        mesh=mesh,
        in_specs=placed,
        out_specs=(P("req", None, "tp"), P("req", None, "tp", None)),
        check_vma=False,
    )
```

```python
import functools
import math

import jax
import jax.numpy as jnp
from jax import lax
from jax.sharding import PartitionSpec as P

HEAD_SIZE = 80


masked_score = -1e30


def turning(positions):
    half_dim = HEAD_SIZE // 2
    frequency = 10000.0 ** (-2.0 * jnp.arange(half_dim, dtype=jnp.float32) / HEAD_SIZE)
    angles = positions.astype(jnp.float32)[..., None] * frequency
    return jnp.cos(angles), jnp.sin(angles)


def rotate(values, cosine_part, sine_part):
    half_dim = HEAD_SIZE // 2
    first_half = values[..., :half_dim]
    second_half = values[..., half_dim:]
    return jnp.concatenate(
        [
            first_half * cosine_part - second_half * sine_part,
            second_half * cosine_part + first_half * sine_part,
        ],
        axis=-1,
    )


def attend(query_rows, key_value_cache, fresh, visible, causal):
    scale = 1.0 / math.sqrt(HEAD_SIZE)
    slot_count = query_rows.shape[0]
    verified = query_rows.shape[1]
    entries = jnp.concatenate([key_value_cache, fresh], axis=1)
    keys = entries[..., :HEAD_SIZE]
    values = entries[..., HEAD_SIZE:]
    seen = jnp.concatenate(
        [
            jnp.broadcast_to(visible[:, None, :], (slot_count, verified, visible.shape[1])),
            jnp.broadcast_to(causal[None, :, :], (slot_count, verified, verified)),
        ],
        axis=2,
    )
    scores = (
        jnp.einsum("rtghd,rcgd->rghtc", query_rows, keys, preferred_element_type=jnp.float32)
        * scale
    )
    scores = jnp.where(seen[:, None, None, :, :], scores, masked_score)
    largest = jnp.max(scores, axis=-1, keepdims=True)
    expos = jnp.exp(scores - largest)
    weights = (expos / jnp.sum(expos, axis=-1, keepdims=True)).astype(jnp.bfloat16)
    mixed = jnp.einsum(
        "rghtc,rcgd->rtghd", weights, values, preferred_element_type=jnp.float32
    )
    return mixed.astype(jnp.bfloat16).reshape(slot_count, verified, -1)


def body(
    hidden,
    norm_gain,
    query_weight,
    key_value_matrix,
    output_weight,
    key_value_cache,
    deal_order,
    cache_length,
    accepted,
    *,
    peers,
    shards,
):
    slot_count = deal_order.shape[0]
    verified = hidden.shape[1]
    width = hidden.shape[2]
    source = deal_order // slot_count
    local = deal_order % slot_count
    match = source[None, :] == jnp.arange(peers, dtype=jnp.int32)[:, None]
    wish = jnp.sum(jnp.where(match, local[None, :] + 1, 0), axis=1) - 1
    wanted = lax.all_to_all(wish.reshape(peers, 1, 1), "req", 0, 0, tiled=True).reshape(peers)
    positions = cache_length[:, None] + jnp.arange(verified, dtype=jnp.int32)[None, :]
    cosine_part, sine_part = turning(positions)
    visible = jnp.arange(key_value_cache.shape[1], dtype=jnp.int32)[None, :] < cache_length[:, None]
    causal = (
        jnp.arange(verified, dtype=jnp.int32)[:, None]
        >= jnp.arange(verified, dtype=jnp.int32)[None, :]
    )
    keep = (jnp.arange(verified, dtype=jnp.int32)[None, :] < accepted[:, None])[:, :, None, None]
    gain = norm_gain.reshape(shards, 1, width).astype(jnp.float32)
    held = (wanted, cosine_part, sine_part, visible, causal, keep, gain)
    (wanted, cosine_part, sine_part, visible, causal, keep, gain) = lax.optimization_barrier(held)
    pick = (wanted[:, None] == jnp.arange(slot_count, dtype=jnp.int32)[None, :]).astype(jnp.bfloat16)
    row_size = verified * width
    tile = 16 * 128
    padded = -(-row_size // tile) * tile
    outgoing = jnp.einsum(
        "dj,jx->dx", pick, hidden.reshape(slot_count, row_size), preferred_element_type=jnp.float32
    ).astype(jnp.bfloat16)
    outgoing = jnp.pad(outgoing, ((0, 0), (0, padded - row_size))).reshape(peers, padded // 128, 128)
    incoming = lax.all_to_all(outgoing, "req", 0, 0, tiled=True)
    incoming = incoming.reshape(peers, padded)[:, :row_size]
    take = match.astype(jnp.bfloat16)
    dealt_rows = jnp.einsum(
        "pi,px->ix", take, incoming, preferred_element_type=jnp.float32
    ).astype(jnp.bfloat16)
    rows = slot_count * verified
    lanes = rows * width // 128
    features = lax.all_gather(dealt_rows.reshape(rows, width), "tp", axis=0, tiled=False)
    widened = features.astype(jnp.float32)
    variance = jnp.mean(widened * widened, axis=(0, 2), keepdims=True)
    normed = (widened * lax.rsqrt(variance + 1e-05) * gain).astype(jnp.bfloat16)
    heads_here = query_weight.shape[1] // HEAD_SIZE
    groups_here = key_value_matrix.shape[1]
    query_rows = jnp.einsum(
        "knf,kfe->ne",
        normed,
        query_weight.reshape(shards, width, -1),
        preferred_element_type=jnp.float32,
    )
    query_rows = query_rows.reshape(
        slot_count, verified, groups_here, heads_here // groups_here, HEAD_SIZE
    )
    query_rows = rotate(query_rows, cosine_part[:, :, None, None], sine_part[:, :, None, None]).astype(jnp.bfloat16)
    projected = jnp.einsum(
        "knf,kfge->nge",
        normed,
        key_value_matrix.reshape(shards, width, groups_here, -1),
        preferred_element_type=jnp.float32,
    ).reshape(slot_count, verified, groups_here, -1)
    fresh = jnp.concatenate(
        [rotate(projected[..., :HEAD_SIZE], cosine_part[:, :, None], sine_part[:, :, None]), projected[..., HEAD_SIZE:]],
        axis=-1,
    ).astype(jnp.bfloat16)
    new_entries = jnp.where(keep, fresh, jnp.zeros_like(fresh))
    mixed = attend(query_rows, key_value_cache, fresh, visible, causal)
    partial_sum = jnp.einsum(
        "ne,ekf->knf",
        mixed.reshape(rows, -1),
        output_weight.reshape(-1, shards, width),
        preferred_element_type=jnp.float32,
    )
    pieces = partial_sum.astype(jnp.bfloat16).reshape(shards, lanes, 128)
    pieces, new_entries = lax.optimization_barrier((pieces, new_entries))
    pieces = lax.all_to_all(pieces, "tp", 0, 0, tiled=True)
    out_dealt = jnp.sum(pieces.astype(jnp.float32), axis=0)
    out_dealt = out_dealt.reshape(slot_count, verified, width).astype(jnp.bfloat16)
    back_out = jnp.einsum(
        "pi,ix->px", take, out_dealt.reshape(slot_count, row_size), preferred_element_type=jnp.float32
    ).astype(jnp.bfloat16)
    back_out = jnp.pad(back_out, ((0, 0), (0, padded - row_size))).reshape(peers, padded // 128, 128)
    returned = lax.all_to_all(back_out, "req", 0, 0, tiled=True)
    returned = returned.reshape(peers, padded)[:, :row_size]
    block_output = jnp.einsum(
        "dj,dx->jx", pick, returned, preferred_element_type=jnp.float32
    ).astype(jnp.bfloat16).reshape(slot_count, verified, width)
    return (block_output, new_entries)


def solution(mesh):
    placed = (
        P("req", None, "tp"),
        P(),
        P(None, "tp"),
        P(None, "tp", None),
        P("tp", None),
        P("req", None, "tp", None),
        P("req"),
        P("req"),
        P("req"),
    )
    return jax.shard_map(
        functools.partial(body, peers=mesh.shape["req"], shards=mesh.shape["tp"]),
        mesh=mesh,
        in_specs=placed,
        out_specs=(P("req", None, "tp"), P("req", None, "tp", None)),
        check_vma=False,
    )
```

```python
import functools
import math

import jax
import jax.numpy as jnp
from jax import lax
from jax.sharding import PartitionSpec as P

HEAD_SIZE = 80


masked_score = -1e30


def turning(positions):
    half_dim = HEAD_SIZE // 2
    frequency = 10000.0 ** (-2.0 * jnp.arange(half_dim, dtype=jnp.float32) / HEAD_SIZE)
    angles = positions.astype(jnp.float32)[..., None] * frequency
    return jnp.cos(angles), jnp.sin(angles)


def rotate(values, cosine_part, sine_part):
    half_dim = HEAD_SIZE // 2
    first_half = values[..., :half_dim]
    second_half = values[..., half_dim:]
    return jnp.concatenate(
        [
            first_half * cosine_part - second_half * sine_part,
            second_half * cosine_part + first_half * sine_part,
        ],
        axis=-1,
    )


def attend(query_rows, key_value_cache, fresh, visible, causal):
    scale = 1.0 / math.sqrt(HEAD_SIZE)
    slot_count = query_rows.shape[0]
    verified = query_rows.shape[1]
    entries = jnp.concatenate([key_value_cache, fresh], axis=1)
    keys = entries[..., :HEAD_SIZE]
    values = entries[..., HEAD_SIZE:]
    seen = jnp.concatenate(
        [
            jnp.broadcast_to(visible[:, None, :], (slot_count, verified, visible.shape[1])),
            jnp.broadcast_to(causal[None, :, :], (slot_count, verified, verified)),
        ],
        axis=2,
    )
    scores = (
        jnp.einsum("rtghd,rcgd->rghtc", query_rows, keys, preferred_element_type=jnp.float32)
        * scale
    )
    scores = jnp.where(seen[:, None, None, :, :], scores, masked_score)
    largest = jnp.max(scores, axis=-1, keepdims=True)
    expos = jnp.exp(scores - largest)
    weights = (expos / jnp.sum(expos, axis=-1, keepdims=True)).astype(jnp.bfloat16)
    mixed = jnp.einsum(
        "rghtc,rcgd->rtghd", weights, values, preferred_element_type=jnp.float32
    )
    return mixed.astype(jnp.bfloat16).reshape(slot_count, verified, -1)


def body(
    hidden,
    norm_gain,
    query_weight,
    key_value_matrix,
    output_weight,
    key_value_cache,
    deal_order,
    cache_length,
    accepted,
    *,
    peers,
    shards,
):
    slot_count = deal_order.shape[0]
    verified = hidden.shape[1]
    width = hidden.shape[2]
    source = deal_order // slot_count
    local = deal_order % slot_count
    match = source[None, :] == jnp.arange(peers, dtype=jnp.int32)[:, None]
    wish = jnp.sum(jnp.where(match, local[None, :] + 1, 0), axis=1) - 1
    wanted = lax.all_to_all(wish.reshape(peers, 1, 1), "req", 0, 0, tiled=True).reshape(peers)
    positions = cache_length[:, None] + jnp.arange(verified, dtype=jnp.int32)[None, :]
    cosine_part, sine_part = turning(positions)
    visible = jnp.arange(key_value_cache.shape[1], dtype=jnp.int32)[None, :] < cache_length[:, None]
    causal = (
        jnp.arange(verified, dtype=jnp.int32)[:, None]
        >= jnp.arange(verified, dtype=jnp.int32)[None, :]
    )
    keep = (jnp.arange(verified, dtype=jnp.int32)[None, :] < accepted[:, None])[:, :, None, None]
    gain = norm_gain.reshape(shards, 1, width).astype(jnp.float32)
    held = (wanted, cosine_part, sine_part, visible, causal, keep, gain)
    (wanted, cosine_part, sine_part, visible, causal, keep, gain) = lax.optimization_barrier(held)
    pick = (wanted[:, None] == jnp.arange(slot_count, dtype=jnp.int32)[None, :]).astype(jnp.bfloat16)
    row_size = verified * width
    tile = 16 * 128
    padded = -(-row_size // tile) * tile
    outgoing = jnp.einsum(
        "dj,jx->dx", pick, hidden.reshape(slot_count, row_size), preferred_element_type=jnp.float32
    ).astype(jnp.bfloat16)
    outgoing = jnp.pad(outgoing, ((0, 0), (0, padded - row_size))).reshape(peers, padded // 128, 128)
    incoming = lax.all_to_all(outgoing, "req", 0, 0, tiled=True)
    incoming = incoming.reshape(peers, padded)[:, :row_size]
    take = match.astype(jnp.bfloat16)
    dealt_rows = jnp.einsum(
        "pi,px->ix", take, incoming, preferred_element_type=jnp.float32
    ).astype(jnp.bfloat16)
    rows = slot_count * verified
    lanes = rows * width // 128
    features = lax.all_gather(dealt_rows.reshape(rows, width), "tp", axis=0, tiled=False)
    widened = features.astype(jnp.float32)
    variance = jnp.mean(widened * widened, axis=(0, 2), keepdims=True)
    normed = (widened * lax.rsqrt(variance + 1e-05) * gain).astype(jnp.bfloat16)
    heads_here = query_weight.shape[1] // HEAD_SIZE
    groups_here = key_value_matrix.shape[1]
    query_rows = jnp.einsum(
        "knf,kfe->ne",
        normed,
        query_weight.reshape(shards, width, -1),
        preferred_element_type=jnp.float32,
    )
    query_rows = query_rows.reshape(
        slot_count, verified, groups_here, heads_here // groups_here, HEAD_SIZE
    )
    query_rows = rotate(query_rows, cosine_part[:, :, None, None], sine_part[:, :, None, None]).astype(jnp.bfloat16)
    projected = jnp.einsum(
        "knf,kfge->nge",
        normed,
        key_value_matrix.reshape(shards, width, groups_here, -1),
        preferred_element_type=jnp.float32,
    ).reshape(slot_count, verified, groups_here, -1)
    fresh = jnp.concatenate(
        [rotate(projected[..., :HEAD_SIZE], cosine_part[:, :, None], sine_part[:, :, None]), projected[..., HEAD_SIZE:]],
        axis=-1,
    ).astype(jnp.bfloat16)
    new_entries = jnp.where(keep, fresh, jnp.zeros_like(fresh))
    mixed = attend(query_rows, key_value_cache, fresh, visible, causal)
    partial_sum = jnp.einsum(
        "ne,ekf->knf",
        mixed.reshape(rows, -1),
        output_weight.reshape(-1, shards, width),
        preferred_element_type=jnp.float32,
    )
    pieces = partial_sum.astype(jnp.bfloat16).reshape(shards, lanes, 128)
    pieces, new_entries = lax.optimization_barrier((pieces, new_entries))
    pieces = lax.all_to_all(pieces, "tp", 0, 0, tiled=True)
    out_dealt = jnp.sum(pieces.astype(jnp.float32), axis=0)
    out_dealt = out_dealt.reshape(slot_count, verified, width).astype(jnp.bfloat16)
    back_out = jnp.einsum(
        "pi,ix->px", take, out_dealt.reshape(slot_count, row_size), preferred_element_type=jnp.float32
    ).astype(jnp.bfloat16)
    back_out = jnp.pad(back_out, ((0, 0), (0, padded - row_size))).reshape(peers, padded // 128, 128)
    returned = lax.all_to_all(back_out, "req", 0, 0, tiled=True)
    returned = returned.reshape(peers, padded)[:, :row_size].reshape(peers, verified, width)
    block_output = jnp.einsum(
        "dj,dtf->tjf", pick, returned, preferred_element_type=jnp.float32
    ).astype(jnp.bfloat16)
    block_output = jnp.transpose(block_output, (1, 0, 2))
    return (block_output, new_entries)


def solution(mesh):
    placed = (
        P("req", None, "tp"),
        P(),
        P(None, "tp"),
        P(None, "tp", None),
        P("tp", None),
        P("req", None, "tp", None),
        P("req"),
        P("req"),
        P("req"),
    )
    return jax.shard_map(
        functools.partial(body, peers=mesh.shape["req"], shards=mesh.shape["tp"]),
        mesh=mesh,
        in_specs=placed,
        out_specs=(P("req", None, "tp"), P("req", None, "tp", None)),
        check_vma=False,
    )
```

```python
import functools
import math

import jax
import jax.numpy as jnp
from jax import lax
from jax.sharding import PartitionSpec as P

HEAD_SIZE = 80


masked_score = -1e30


def turning(positions):
    half_dim = HEAD_SIZE // 2
    frequency = 10000.0 ** (-2.0 * jnp.arange(half_dim, dtype=jnp.float32) / HEAD_SIZE)
    angles = positions.astype(jnp.float32)[..., None] * frequency
    return jnp.cos(angles), jnp.sin(angles)


def rotate(values, cosine_part, sine_part):
    half_dim = HEAD_SIZE // 2
    first_half = values[..., :half_dim]
    second_half = values[..., half_dim:]
    return jnp.concatenate(
        [
            first_half * cosine_part - second_half * sine_part,
            second_half * cosine_part + first_half * sine_part,
        ],
        axis=-1,
    )


def attend(query_rows, key_value_cache, fresh, visible, causal):
    scale = 1.0 / math.sqrt(HEAD_SIZE)
    slot_count = query_rows.shape[0]
    verified = query_rows.shape[1]
    entries = jnp.concatenate([key_value_cache, fresh], axis=1)
    keys = entries[..., :HEAD_SIZE]
    values = entries[..., HEAD_SIZE:]
    seen = jnp.concatenate(
        [
            jnp.broadcast_to(visible[:, None, :], (slot_count, verified, visible.shape[1])),
            jnp.broadcast_to(causal[None, :, :], (slot_count, verified, verified)),
        ],
        axis=2,
    )
    scores = (
        jnp.einsum("rtghd,rcgd->rghtc", query_rows, keys, preferred_element_type=jnp.float32)
        * scale
    )
    scores = jnp.where(seen[:, None, None, :, :], scores, masked_score)
    largest = jnp.max(scores, axis=-1, keepdims=True)
    expos = jnp.exp(scores - largest)
    weights = (expos / jnp.sum(expos, axis=-1, keepdims=True)).astype(jnp.bfloat16)
    mixed = jnp.einsum(
        "rghtc,rcgd->rtghd", weights, values, preferred_element_type=jnp.float32
    )
    return mixed.astype(jnp.bfloat16).reshape(slot_count, verified, -1)


def body(
    hidden,
    norm_gain,
    query_weight,
    key_value_matrix,
    output_weight,
    key_value_cache,
    deal_order,
    cache_length,
    accepted,
    *,
    peers,
    shards,
):
    slot_count = deal_order.shape[0]
    verified = hidden.shape[1]
    width = hidden.shape[2]
    if slot_count & (slot_count - 1) == 0:
        source = lax.shift_right_logical(deal_order, slot_count.bit_length() - 1)
        local = lax.bitwise_and(deal_order, slot_count - 1)
    else:
        source = deal_order // slot_count
        local = deal_order % slot_count
    match = source[None, :] == jnp.arange(peers, dtype=jnp.int32)[:, None]
    wish = jnp.sum(jnp.where(match, local[None, :] + 1, 0), axis=1) - 1
    wanted = lax.all_to_all(wish.reshape(peers, 1, 1), "req", 0, 0, tiled=True).reshape(peers)
    positions = cache_length[:, None] + jnp.arange(verified, dtype=jnp.int32)[None, :]
    cosine_part, sine_part = turning(positions)
    visible = jnp.arange(key_value_cache.shape[1], dtype=jnp.int32)[None, :] < cache_length[:, None]
    causal = (
        jnp.arange(verified, dtype=jnp.int32)[:, None]
        >= jnp.arange(verified, dtype=jnp.int32)[None, :]
    )
    keep = (jnp.arange(verified, dtype=jnp.int32)[None, :] < accepted[:, None])[:, :, None, None]
    gain = norm_gain.reshape(shards, 1, width).astype(jnp.float32)
    held = (wanted, cosine_part, sine_part, visible, causal, keep, gain)
    (wanted, cosine_part, sine_part, visible, causal, keep, gain) = lax.optimization_barrier(held)
    pick = (wanted[:, None] == jnp.arange(slot_count, dtype=jnp.int32)[None, :]).astype(jnp.bfloat16)
    row_size = verified * width
    tile = 16 * 128
    padded = -(-row_size // tile) * tile
    outgoing = jnp.einsum(
        "dj,jx->dx", pick, hidden.reshape(slot_count, row_size), preferred_element_type=jnp.float32
    ).astype(jnp.bfloat16)
    outgoing = jnp.pad(outgoing, ((0, 0), (0, padded - row_size))).reshape(peers, padded // 128, 128)
    incoming = lax.all_to_all(outgoing, "req", 0, 0, tiled=True)
    incoming = incoming.reshape(peers, padded)[:, :row_size]
    take = match.astype(jnp.bfloat16)
    dealt_rows = jnp.einsum(
        "pi,px->ix", take, incoming, preferred_element_type=jnp.float32
    ).astype(jnp.bfloat16)
    rows = slot_count * verified
    lanes = rows * width // 128
    features = lax.all_gather(dealt_rows.reshape(rows, width), "tp", axis=0, tiled=False)
    widened = features.astype(jnp.float32)
    variance = jnp.mean(widened * widened, axis=(0, 2), keepdims=True)
    normed = (widened * lax.rsqrt(variance + 1e-05) * gain).astype(jnp.bfloat16)
    heads_here = query_weight.shape[1] // HEAD_SIZE
    groups_here = key_value_matrix.shape[1]
    query_rows = jnp.einsum(
        "knf,kfe->ne",
        normed,
        query_weight.reshape(shards, width, -1),
        preferred_element_type=jnp.float32,
    )
    query_rows = query_rows.reshape(
        slot_count, verified, groups_here, heads_here // groups_here, HEAD_SIZE
    )
    query_rows = rotate(query_rows, cosine_part[:, :, None, None], sine_part[:, :, None, None]).astype(jnp.bfloat16)
    projected = jnp.einsum(
        "knf,kfge->nge",
        normed,
        key_value_matrix.reshape(shards, width, groups_here, -1),
        preferred_element_type=jnp.float32,
    ).reshape(slot_count, verified, groups_here, -1)
    fresh = jnp.concatenate(
        [rotate(projected[..., :HEAD_SIZE], cosine_part[:, :, None], sine_part[:, :, None]), projected[..., HEAD_SIZE:]],
        axis=-1,
    ).astype(jnp.bfloat16)
    new_entries = jnp.where(keep, fresh, jnp.zeros_like(fresh))
    mixed = attend(query_rows, key_value_cache, fresh, visible, causal)
    partial_sum = jnp.einsum(
        "ne,ekf->knf",
        mixed.reshape(rows, -1),
        output_weight.reshape(-1, shards, width),
        preferred_element_type=jnp.float32,
    )
    pieces = partial_sum.astype(jnp.bfloat16).reshape(shards, lanes, 128)
    pieces, new_entries = lax.optimization_barrier((pieces, new_entries))
    pieces = lax.all_to_all(pieces, "tp", 0, 0, tiled=True)
    out_dealt = jnp.sum(pieces.astype(jnp.float32), axis=0)
    out_dealt = out_dealt.reshape(slot_count, verified, width).astype(jnp.bfloat16)
    back_out = jnp.einsum(
        "pi,ix->px", take, out_dealt.reshape(slot_count, row_size), preferred_element_type=jnp.float32
    ).astype(jnp.bfloat16)
    back_out = jnp.pad(back_out, ((0, 0), (0, padded - row_size))).reshape(peers, padded // 128, 128)
    returned = lax.all_to_all(back_out, "req", 0, 0, tiled=True)
    returned = returned.reshape(peers, padded)[:, :row_size]
    block_output = jnp.einsum(
        "dj,dx->jx", pick, returned, preferred_element_type=jnp.float32
    ).astype(jnp.bfloat16).reshape(slot_count, verified, width)
    return (block_output, new_entries)


def solution(mesh):
    placed = (
        P("req", None, "tp"),
        P(),
        P(None, "tp"),
        P(None, "tp", None),
        P("tp", None),
        P("req", None, "tp", None),
        P("req"),
        P("req"),
        P("req"),
    )
    return jax.shard_map(
        functools.partial(body, peers=mesh.shape["req"], shards=mesh.shape["tp"]),
        mesh=mesh,
        in_specs=placed,
        out_specs=(P("req", None, "tp"), P("req", None, "tp", None)),
        check_vma=False,
    )
```

```python
import functools
import math

import jax
import jax.numpy as jnp
from jax import lax
from jax.sharding import PartitionSpec as P

HEAD_SIZE = 80


masked_score = -1e30


def turning(positions):
    half_dim = HEAD_SIZE // 2
    frequency = 10000.0 ** (-2.0 * jnp.arange(half_dim, dtype=jnp.float32) / HEAD_SIZE)
    angles = positions.astype(jnp.float32)[..., None] * frequency
    return jnp.cos(angles), jnp.sin(angles)


def rotate(values, cosine_part, sine_part):
    half_dim = HEAD_SIZE // 2
    first_half = values[..., :half_dim]
    second_half = values[..., half_dim:]
    return jnp.concatenate(
        [
            first_half * cosine_part - second_half * sine_part,
            second_half * cosine_part + first_half * sine_part,
        ],
        axis=-1,
    )


def attend(query_rows, key_value_cache, fresh, visible, causal):
    scale = 1.0 / math.sqrt(HEAD_SIZE)
    slot_count = query_rows.shape[0]
    verified = query_rows.shape[1]
    entries = jnp.concatenate([key_value_cache, fresh], axis=1)
    keys = entries[..., :HEAD_SIZE]
    values = entries[..., HEAD_SIZE:]
    seen = jnp.concatenate(
        [
            jnp.broadcast_to(visible[:, None, :], (slot_count, verified, visible.shape[1])),
            jnp.broadcast_to(causal[None, :, :], (slot_count, verified, verified)),
        ],
        axis=2,
    )
    scores = (
        jnp.einsum("rtghd,rcgd->rghtc", query_rows, keys, preferred_element_type=jnp.float32)
        * scale
    )
    scores = jnp.where(seen[:, None, None, :, :], scores, masked_score)
    largest = jnp.max(scores, axis=-1, keepdims=True)
    expos = jnp.exp(scores - largest)
    weights = (expos / jnp.sum(expos, axis=-1, keepdims=True)).astype(jnp.bfloat16)
    mixed = jnp.einsum(
        "rghtc,rcgd->rtghd", weights, values, preferred_element_type=jnp.float32
    )
    return mixed.astype(jnp.bfloat16).reshape(slot_count, verified, -1)


def body(
    hidden,
    norm_gain,
    query_weight,
    key_value_matrix,
    output_weight,
    key_value_cache,
    deal_order,
    cache_length,
    accepted,
    *,
    peers,
    shards,
):
    slot_count = deal_order.shape[0]
    verified = hidden.shape[1]
    width = hidden.shape[2]
    source = deal_order // slot_count
    local = deal_order % slot_count
    match = source[None, :] == jnp.arange(peers, dtype=jnp.int32)[:, None]
    wish = jnp.sum(jnp.where(match, local[None, :] + 1, 0), axis=1) - 1
    wanted = lax.all_to_all(wish.reshape(peers, 1, 1), "req", 0, 0, tiled=True).reshape(peers)
    positions = cache_length[:, None] + jnp.arange(verified, dtype=jnp.int32)[None, :]
    cosine_part, sine_part = turning(positions)
    visible = jnp.arange(key_value_cache.shape[1], dtype=jnp.int32)[None, :] < cache_length[:, None]
    causal = (
        jnp.arange(verified, dtype=jnp.int32)[:, None]
        >= jnp.arange(verified, dtype=jnp.int32)[None, :]
    )
    keep = (jnp.arange(verified, dtype=jnp.int32)[None, :] < accepted[:, None])[:, :, None, None]
    gain = norm_gain.reshape(shards, 1, width).astype(jnp.float32)
    held = (wanted, cosine_part, sine_part, visible, causal, keep, gain)
    (wanted, cosine_part, sine_part, visible, causal, keep, gain) = lax.optimization_barrier(held)
    pick = (wanted[:, None] == jnp.arange(slot_count, dtype=jnp.int32)[None, :]).astype(jnp.bfloat16)
    row_size = verified * width
    tile = 16 * 128
    padded = -(-row_size // tile) * tile
    outgoing = jnp.einsum(
        "dj,jx->dx", pick, hidden.reshape(slot_count, row_size), preferred_element_type=jnp.float32
    ).astype(jnp.bfloat16)
    outgoing = jnp.pad(outgoing, ((0, 0), (0, padded - row_size))).reshape(peers, padded // 128, 128)
    incoming = lax.all_to_all(outgoing, "req", 0, 0, tiled=True)
    incoming = incoming.reshape(peers, padded)[:, :row_size]
    take = match.astype(jnp.bfloat16)
    dealt_rows = jnp.einsum(
        "pi,px->ix", take, incoming, preferred_element_type=jnp.float32
    ).astype(jnp.bfloat16)
    rows = slot_count * verified
    lanes = rows * width // 128
    features = lax.all_gather(dealt_rows.reshape(rows, width), "tp", axis=0, tiled=False)
    widened = features.astype(jnp.float32)
    variance = jnp.mean(widened * widened, axis=(0, 2), keepdims=True)
    normed = (widened * lax.rsqrt(variance + 1e-05) * gain).astype(jnp.bfloat16)
    heads_here = query_weight.shape[1] // HEAD_SIZE
    groups_here = key_value_matrix.shape[1]
    both_weights = jnp.concatenate(
        [query_weight.reshape(shards, width, -1), key_value_matrix.reshape(shards, width, -1)], axis=2
    )
    both_rows = jnp.einsum("knf,kfe->ne", normed, both_weights, preferred_element_type=jnp.float32)
    query_rows = both_rows[:, : query_weight.shape[1]]
    query_rows = query_rows.reshape(
        slot_count, verified, groups_here, heads_here // groups_here, HEAD_SIZE
    )
    query_rows = rotate(query_rows, cosine_part[:, :, None, None], sine_part[:, :, None, None]).astype(jnp.bfloat16)
    projected = both_rows[:, query_weight.shape[1] :].reshape(slot_count, verified, groups_here, -1)
    fresh = jnp.concatenate(
        [rotate(projected[..., :HEAD_SIZE], cosine_part[:, :, None], sine_part[:, :, None]), projected[..., HEAD_SIZE:]],
        axis=-1,
    ).astype(jnp.bfloat16)
    new_entries = jnp.where(keep, fresh, jnp.zeros_like(fresh))
    mixed = attend(query_rows, key_value_cache, fresh, visible, causal)
    partial_sum = jnp.einsum(
        "ne,ekf->knf",
        mixed.reshape(rows, -1),
        output_weight.reshape(-1, shards, width),
        preferred_element_type=jnp.float32,
    )
    pieces = partial_sum.astype(jnp.bfloat16).reshape(shards, lanes, 128)
    pieces, new_entries = lax.optimization_barrier((pieces, new_entries))
    pieces = lax.all_to_all(pieces, "tp", 0, 0, tiled=True)
    out_dealt = jnp.sum(pieces.astype(jnp.float32), axis=0)
    out_dealt = out_dealt.reshape(slot_count, verified, width).astype(jnp.bfloat16)
    back_out = jnp.einsum(
        "pi,ix->px", take, out_dealt.reshape(slot_count, row_size), preferred_element_type=jnp.float32
    ).astype(jnp.bfloat16)
    back_out = jnp.pad(back_out, ((0, 0), (0, padded - row_size))).reshape(peers, padded // 128, 128)
    returned = lax.all_to_all(back_out, "req", 0, 0, tiled=True)
    returned = returned.reshape(peers, padded)[:, :row_size]
    block_output = jnp.einsum(
        "dj,dx->jx", pick, returned, preferred_element_type=jnp.float32
    ).astype(jnp.bfloat16).reshape(slot_count, verified, width)
    return (block_output, new_entries)


def solution(mesh):
    placed = (
        P("req", None, "tp"),
        P(),
        P(None, "tp"),
        P(None, "tp", None),
        P("tp", None),
        P("req", None, "tp", None),
        P("req"),
        P("req"),
        P("req"),
    )
    return jax.shard_map(
        functools.partial(body, peers=mesh.shape["req"], shards=mesh.shape["tp"]),
        mesh=mesh,
        in_specs=placed,
        out_specs=(P("req", None, "tp"), P("req", None, "tp", None)),
        check_vma=False,
    )
```

```python
import functools
import math

import jax
import jax.numpy as jnp
from jax import lax
from jax.sharding import PartitionSpec as P

HEAD_SIZE = 80


masked_score = -1e30


def turning(positions):
    half_dim = HEAD_SIZE // 2
    frequency = 10000.0 ** (-2.0 * jnp.arange(half_dim, dtype=jnp.float32) / HEAD_SIZE)
    angles = positions.astype(jnp.float32)[..., None] * frequency
    return jnp.cos(angles), jnp.sin(angles)


def rotate(values, cosine_part, sine_part):
    half_dim = HEAD_SIZE // 2
    first_half = values[..., :half_dim]
    second_half = values[..., half_dim:]
    return jnp.concatenate(
        [
            first_half * cosine_part - second_half * sine_part,
            second_half * cosine_part + first_half * sine_part,
        ],
        axis=-1,
    )


def attend(query_rows, key_value_cache, fresh, visible, causal):
    scale = 1.0 / math.sqrt(HEAD_SIZE)
    slot_count = query_rows.shape[0]
    verified = query_rows.shape[1]
    entries = jnp.concatenate([key_value_cache, fresh], axis=1)
    keys = entries[..., :HEAD_SIZE]
    values = entries[..., HEAD_SIZE:]
    seen = jnp.concatenate(
        [
            jnp.broadcast_to(visible[:, None, :], (slot_count, verified, visible.shape[1])),
            jnp.broadcast_to(causal[None, :, :], (slot_count, verified, verified)),
        ],
        axis=2,
    )
    scores = (
        jnp.einsum("rtghd,rcgd->rghtc", query_rows, keys, preferred_element_type=jnp.float32)
        * scale
    )
    scores = jnp.where(seen[:, None, None, :, :], scores, masked_score)
    largest = jnp.max(scores, axis=-1, keepdims=True)
    expos = jnp.exp(scores - largest)
    weights = (expos / jnp.sum(expos, axis=-1, keepdims=True)).astype(jnp.bfloat16)
    mixed = jnp.einsum(
        "rghtc,rcgd->rtghd", weights, values, preferred_element_type=jnp.float32
    )
    return mixed.astype(jnp.bfloat16).reshape(slot_count, verified, -1)


def body(
    hidden,
    norm_gain,
    query_weight,
    key_value_matrix,
    output_weight,
    key_value_cache,
    deal_order,
    cache_length,
    accepted,
    *,
    peers,
    shards,
):
    slot_count = deal_order.shape[0]
    verified = hidden.shape[1]
    width = hidden.shape[2]
    source = deal_order // slot_count
    local = deal_order % slot_count
    match = source[None, :] == jnp.arange(peers, dtype=jnp.int32)[:, None]
    wish = jnp.sum(jnp.where(match, local[None, :] + 1, 0), axis=1) - 1
    wanted = lax.all_to_all(wish.reshape(peers, 1, 1), "req", 0, 0, tiled=True).reshape(peers)
    positions = cache_length[:, None] + jnp.arange(verified, dtype=jnp.int32)[None, :]
    cosine_part, sine_part = turning(positions)
    visible = jnp.arange(key_value_cache.shape[1], dtype=jnp.int32)[None, :] < cache_length[:, None]
    causal = (
        jnp.arange(verified, dtype=jnp.int32)[:, None]
        >= jnp.arange(verified, dtype=jnp.int32)[None, :]
    )
    keep = (jnp.arange(verified, dtype=jnp.int32)[None, :] < accepted[:, None])[:, :, None, None]
    gain = norm_gain.reshape(shards, 1, width).astype(jnp.float32)
    held = (wanted, cosine_part, sine_part, visible, causal, keep, gain)
    (wanted, cosine_part, sine_part, visible, causal, keep, gain) = lax.optimization_barrier(held)
    pick = (wanted[:, None] == jnp.arange(slot_count, dtype=jnp.int32)[None, :]).astype(jnp.bfloat16)
    row_size = verified * width
    tile = 16 * 128
    padded = -(-row_size // tile) * tile
    outgoing = jnp.einsum(
        "dj,jx->dx", pick, hidden.reshape(slot_count, row_size), preferred_element_type=jnp.float32
    ).astype(jnp.bfloat16)
    outgoing = jnp.pad(outgoing, ((0, 0), (0, padded - row_size))).reshape(peers, padded // 128, 128)
    incoming = lax.all_to_all(outgoing, "req", 0, 0, tiled=True)
    incoming = incoming.reshape(peers, padded)
    take = match.astype(jnp.bfloat16)
    dealt_rows = jnp.einsum(
        "pi,px->ix", take, incoming, preferred_element_type=jnp.float32
    ).astype(jnp.bfloat16)[:, :row_size]
    rows = slot_count * verified
    lanes = rows * width // 128
    features = lax.all_gather(dealt_rows.reshape(rows, width), "tp", axis=0, tiled=False)
    widened = features.astype(jnp.float32)
    variance = jnp.mean(widened * widened, axis=(0, 2), keepdims=True)
    normed = (widened * lax.rsqrt(variance + 1e-05) * gain).astype(jnp.bfloat16)
    heads_here = query_weight.shape[1] // HEAD_SIZE
    groups_here = key_value_matrix.shape[1]
    query_rows = jnp.einsum(
        "knf,kfe->ne",
        normed,
        query_weight.reshape(shards, width, -1),
        preferred_element_type=jnp.float32,
    )
    query_rows = query_rows.reshape(
        slot_count, verified, groups_here, heads_here // groups_here, HEAD_SIZE
    )
    query_rows = rotate(query_rows, cosine_part[:, :, None, None], sine_part[:, :, None, None]).astype(jnp.bfloat16)
    projected = jnp.einsum(
        "knf,kfge->nge",
        normed,
        key_value_matrix.reshape(shards, width, groups_here, -1),
        preferred_element_type=jnp.float32,
    ).reshape(slot_count, verified, groups_here, -1)
    fresh = jnp.concatenate(
        [rotate(projected[..., :HEAD_SIZE], cosine_part[:, :, None], sine_part[:, :, None]), projected[..., HEAD_SIZE:]],
        axis=-1,
    ).astype(jnp.bfloat16)
    new_entries = jnp.where(keep, fresh, jnp.zeros_like(fresh))
    mixed = attend(query_rows, key_value_cache, fresh, visible, causal)
    partial_sum = jnp.einsum(
        "ne,ekf->knf",
        mixed.reshape(rows, -1),
        output_weight.reshape(-1, shards, width),
        preferred_element_type=jnp.float32,
    )
    pieces = partial_sum.astype(jnp.bfloat16).reshape(shards, lanes, 128)
    pieces, new_entries = lax.optimization_barrier((pieces, new_entries))
    pieces = lax.all_to_all(pieces, "tp", 0, 0, tiled=True)
    out_dealt = jnp.sum(pieces.astype(jnp.float32), axis=0)
    out_dealt = out_dealt.reshape(slot_count, verified, width).astype(jnp.bfloat16)
    back_out = jnp.einsum(
        "pi,ix->px", take, out_dealt.reshape(slot_count, row_size), preferred_element_type=jnp.float32
    ).astype(jnp.bfloat16)
    back_out = jnp.pad(back_out, ((0, 0), (0, padded - row_size))).reshape(peers, padded // 128, 128)
    returned = lax.all_to_all(back_out, "req", 0, 0, tiled=True)
    returned = returned.reshape(peers, padded)[:, :row_size]
    block_output = jnp.einsum(
        "dj,dx->jx", pick, returned, preferred_element_type=jnp.float32
    ).astype(jnp.bfloat16).reshape(slot_count, verified, width)
    return (block_output, new_entries)


def solution(mesh):
    placed = (
        P("req", None, "tp"),
        P(),
        P(None, "tp"),
        P(None, "tp", None),
        P("tp", None),
        P("req", None, "tp", None),
        P("req"),
        P("req"),
        P("req"),
    )
    return jax.shard_map(
        functools.partial(body, peers=mesh.shape["req"], shards=mesh.shape["tp"]),
        mesh=mesh,
        in_specs=placed,
        out_specs=(P("req", None, "tp"), P("req", None, "tp", None)),
        check_vma=False,
    )
```

```python
import functools
import math

import jax
import jax.numpy as jnp
from jax import lax
from jax.sharding import PartitionSpec as P

HEAD_SIZE = 80


masked_score = -1e30


def turning(positions):
    half_dim = HEAD_SIZE // 2
    frequency = 10000.0 ** (-2.0 * jnp.arange(half_dim, dtype=jnp.float32) / HEAD_SIZE)
    angles = positions.astype(jnp.float32)[..., None] * frequency
    return jnp.cos(angles), jnp.sin(angles)


def rotate(values, cosine_part, sine_part):
    half_dim = HEAD_SIZE // 2
    first_half = values[..., :half_dim]
    second_half = values[..., half_dim:]
    return jnp.concatenate(
        [
            first_half * cosine_part - second_half * sine_part,
            second_half * cosine_part + first_half * sine_part,
        ],
        axis=-1,
    )


def attend(query_rows, key_value_cache, fresh, visible, causal):
    scale = 1.0 / math.sqrt(HEAD_SIZE)
    slot_count = query_rows.shape[0]
    verified = query_rows.shape[1]
    entries = jnp.concatenate([key_value_cache, fresh], axis=1)
    keys = entries[..., :HEAD_SIZE]
    values = entries[..., HEAD_SIZE:]
    seen = jnp.concatenate(
        [
            jnp.broadcast_to(visible[:, None, :], (slot_count, verified, visible.shape[1])),
            jnp.broadcast_to(causal[None, :, :], (slot_count, verified, verified)),
        ],
        axis=2,
    )
    scores = (
        jnp.einsum("rtghd,rcgd->rghtc", query_rows, keys, preferred_element_type=jnp.float32)
        * scale
    )
    scores = jnp.where(seen[:, None, None, :, :], scores, masked_score)
    largest = jnp.max(scores, axis=-1, keepdims=True)
    expos = jnp.exp(scores - largest)
    weights = (expos / jnp.sum(expos, axis=-1, keepdims=True)).astype(jnp.bfloat16)
    mixed = jnp.einsum(
        "rghtc,rcgd->rtghd", weights, values, preferred_element_type=jnp.float32
    )
    return mixed.astype(jnp.bfloat16).reshape(slot_count, verified, -1)


def body(
    hidden,
    norm_gain,
    query_weight,
    key_value_matrix,
    output_weight,
    key_value_cache,
    deal_order,
    cache_length,
    accepted,
    *,
    peers,
    shards,
):
    slot_count = deal_order.shape[0]
    verified = hidden.shape[1]
    width = hidden.shape[2]
    source = deal_order // slot_count
    local = deal_order % slot_count
    match = source[None, :] == jnp.arange(peers, dtype=jnp.int32)[:, None]
    wish = jnp.sum(jnp.where(match, local[None, :] + 1, 0), axis=1) - 1
    wanted = lax.all_to_all(wish.reshape(peers, 1, 1), "req", 0, 0, tiled=True).reshape(peers)
    positions = cache_length[:, None] + jnp.arange(verified, dtype=jnp.int32)[None, :]
    cosine_part, sine_part = turning(positions)
    visible = jnp.arange(key_value_cache.shape[1], dtype=jnp.int32)[None, :] < cache_length[:, None]
    causal = (
        jnp.arange(verified, dtype=jnp.int32)[:, None]
        >= jnp.arange(verified, dtype=jnp.int32)[None, :]
    )
    keep = (jnp.arange(verified, dtype=jnp.int32)[None, :] < accepted[:, None])[:, :, None, None]
    gain = norm_gain.reshape(shards, 1, width).astype(jnp.float32)
    held = (wanted, cosine_part, sine_part, visible, causal, keep, gain)
    (wanted, cosine_part, sine_part, visible, causal, keep, gain) = lax.optimization_barrier(held)
    pick = (wanted[:, None] == jnp.arange(slot_count, dtype=jnp.int32)[None, :]).astype(jnp.bfloat16)
    row_size = verified * width
    tile = 16 * 128
    padded = -(-row_size // tile) * tile
    outgoing = jnp.einsum(
        "dj,jx->dx", pick, hidden.reshape(slot_count, row_size), preferred_element_type=jnp.float32
    ).astype(jnp.bfloat16)
    outgoing = jnp.pad(outgoing, ((0, 0), (0, padded - row_size))).reshape(peers, padded // 128, 128)
    incoming = lax.all_to_all(outgoing, "req", 0, 0, tiled=True)
    incoming = incoming.reshape(peers, padded)[:, :row_size]
    take = match.astype(jnp.bfloat16)
    dealt_rows = jnp.einsum(
        "pi,px->ix", take, incoming, preferred_element_type=jnp.float32
    ).astype(jnp.bfloat16)
    rows = slot_count * verified
    lanes = rows * width // 128
    features = lax.all_gather(dealt_rows.reshape(rows, width), "tp", axis=0, tiled=False)
    widened = features.astype(jnp.float32)
    variance = jnp.mean(widened * widened, axis=(0, 2), keepdims=True)
    normed = (widened * lax.rsqrt(variance + 1e-05) * gain).astype(jnp.bfloat16)
    heads_here = query_weight.shape[1] // HEAD_SIZE
    groups_here = key_value_matrix.shape[1]
    query_rows = jnp.einsum(
        "knf,kfe->ne",
        normed,
        query_weight.reshape(shards, width, -1),
        preferred_element_type=jnp.float32,
    )
    query_rows = query_rows.reshape(
        slot_count, verified, groups_here, heads_here // groups_here, HEAD_SIZE
    )
    query_rows = rotate(query_rows, cosine_part[:, :, None, None], sine_part[:, :, None, None]).astype(jnp.bfloat16)
    projected = jnp.einsum(
        "knf,kfge->nge",
        normed,
        key_value_matrix.reshape(shards, width, groups_here, -1),
        preferred_element_type=jnp.float32,
    ).reshape(slot_count, verified, groups_here, -1)
    fresh = jnp.concatenate(
        [rotate(projected[..., :HEAD_SIZE], cosine_part[:, :, None], sine_part[:, :, None]), projected[..., HEAD_SIZE:]],
        axis=-1,
    ).astype(jnp.bfloat16)
    new_entries = jnp.where(keep, fresh, jnp.zeros_like(fresh))
    mixed = attend(query_rows, key_value_cache, fresh, visible, causal)
    partial_sum = jnp.einsum(
        "ne,ekf->knf",
        mixed.reshape(rows, -1),
        output_weight.reshape(-1, shards, width),
        preferred_element_type=jnp.float32,
    )
    pieces = partial_sum.astype(jnp.bfloat16).reshape(shards, lanes, 128)
    pieces, new_entries = lax.optimization_barrier((pieces, new_entries))
    pieces = lax.all_to_all(pieces, "tp", 0, 0, tiled=True)
    out_dealt = jnp.sum(pieces.astype(jnp.float32), axis=0)
    out_dealt = out_dealt.reshape(slot_count, verified, width).astype(jnp.bfloat16)
    back_out = jnp.einsum(
        "pi,ix->px", take, out_dealt.reshape(slot_count, row_size), preferred_element_type=jnp.float32
    ).astype(jnp.bfloat16)
    back_out = jnp.pad(back_out, ((0, 0), (0, padded - row_size))).reshape(peers, padded // 128, 128)
    returned = lax.all_to_all(back_out, "req", 0, 0, tiled=True)
    returned = returned.reshape(peers, padded)
    block_output = jnp.einsum(
        "dj,dx->jx", pick, returned, preferred_element_type=jnp.float32
    ).astype(jnp.bfloat16)[:, :row_size].reshape(slot_count, verified, width)
    return (block_output, new_entries)


def solution(mesh):
    placed = (
        P("req", None, "tp"),
        P(),
        P(None, "tp"),
        P(None, "tp", None),
        P("tp", None),
        P("req", None, "tp", None),
        P("req"),
        P("req"),
        P("req"),
    )
    return jax.shard_map(
        functools.partial(body, peers=mesh.shape["req"], shards=mesh.shape["tp"]),
        mesh=mesh,
        in_specs=placed,
        out_specs=(P("req", None, "tp"), P("req", None, "tp", None)),
        check_vma=False,
    )
```
